128 devices in a mesh: rad: 4 (over x_hi, core), sec: 32 (over x_lo, y, z).
Axes of the slice: x: 4 (x_hi: 2, x_lo: 2; x = x_hi * 2 + x_lo), y: 4, z: 4, core: 2. Of those that a mesh axis runs over, the one named last changes fastest.
Arguments:
- gas_fields: float32 [5, 128, 16, 8192], P(None, 'rad', None, 'sec'), may hold values from -8 to 8, as said below
- orbit_shift: int32 [128], P('rad'), may hold values from 0 to 8191
- particle_velocity: float32 [3, 524288], P(None, ('rad', 'sec')), may hold values from -6 to 6
- particle_mass: float32 [524288], P(('rad', 'sec')), may hold values from 0.2 to 2
- particle_stop: float32 [524288], P(('rad', 'sec')), may hold values from 0.1 to 10
- particle_cell: int32 [524288], P(('rad', 'sec')), may hold values from 0 to 131071
- particle_dest: int32 [524288, 1], P(('rad', 'sec')), may hold values from 0 to 127; in each aligned block of 4096 rows (0 to 4095, 4096 to 8191, ...) at most 64 rows name the same one
Outputs:
- gas_next: float32 [5, 128, 16, 8192], P(None, 'rad', None, 'sec')
- arrived_velocity: float32 [3, 1048576], P(None, ('rad', 'sec'))
The draws below stay inside these ranges and needn't reach their ends.
Inputs may be any that keep to these rules, and one draw needn't show every extreme that they name: `gas_fields`: field 0 (density) lies between 0.25 and 4 and momentum over density between -2 and 2. `particle_dest`: among the 4096 particles of one device at most 64 name the same destination; in every draw some device sends exactly 64 to one destination.
All inputs are finite; a program needn't handle non-finite values.
Results may differ from the reference program's by a relative error of at most 0.0003.
Values sent between devices are 32-bit elements; how exact they have to be, the bound alone decides.
No kernel may reach another device: no remote copies, remote signals or barrier semaphores. Data moves between devices by JAX's collectives and lax.ppermute only.
A program may use at most 128 MiB of HBM per device.

```python
import math
import jax
import jax.numpy as jnp
import numpy as np
from jax import lax

CR = 32
ZL = 16
CP = 256
PD = 4096
NR = 128
NPHI = 8192
CAP = 64
NPART = 524288
N_SEC = 32
DEVICES = 128


def draw_gas_fields(key, part):
    subkeys = jax.random.split(key, 3)
    grid_shape = (1, NR, ZL, NPHI)
    motion_shape = (3, NR, ZL, NPHI)
    density = jnp.exp(jax.random.uniform(subkeys[0], grid_shape, jnp.float32, -0.7, 0.7))
    motion = jnp.clip(0.5 * jax.random.normal(subkeys[1], motion_shape, jnp.float32), -2.0, 2.0) * density
    energy = jnp.exp(jax.random.uniform(subkeys[2], grid_shape, jnp.float32, 0.0, 1.1))
    return jnp.concatenate([density, motion, energy], axis=0)


def place_ends(result, stream_key, low, top_value):
    shape = result.shape
    index_at = [jax.random.randint(jax.random.fold_in(stream_key, axis), (), 0, shape[axis]) for axis in range(len(shape))]
    result = result.at[tuple(index_at)].set(low)
    longest = shape.index(max(shape))
    index_at[longest] = (index_at[longest] + 1) % shape[longest]
    return result.at[tuple(index_at)].set(top_value)


def level_of(stream_key, shape, cuts, least, largest):
    factor_of = 1.0
    for position, blocks in cuts:
        heights = jax.random.uniform(jax.random.fold_in(jax.random.fold_in(stream_key, 6), position), (blocks,), jnp.float32, least / len(cuts), largest / len(cuts))
        factor_of = factor_of * jnp.repeat(jnp.exp(heights), shape[position] // blocks).reshape((-1,) + (1,) * (len(shape) - 1 - position))
    return factor_of


def routed_block(own_key, own, number, rows, number_of, top, most, slope):
    sequence = jax.random.permutation(own_key, number_of)
    crowded, ordinary = shares(number_of, rows * top, most, slope, True), shares(number_of, rows * top, most, slope, False)
    places = jnp.arange(number_of)

    def named(tallies, rotation):
        used = int((tallies > 0).sum())
        fixed = max(1, used // 4)
        moved = fixed + (places - fixed + rotation * (used - fixed)) % max(1, number_of - fixed)
        return jnp.zeros((number_of,), jnp.int32).at[sequence[jnp.where(places < fixed, places, moved)]].set(jnp.asarray(tallies, jnp.int32))

    tallies = jnp.where(number % 4 == 0, named(crowded, number // 4), named(ordinary, number - number // 4 - 1))
    mixed = jax.random.permutation(jax.random.fold_in(own, 3), number_of)
    donor, sink = mixed[0:number_of // 2 * 2:2], mixed[1:number_of // 2 * 2:2]
    margin = jnp.minimum(tallies[donor] - 1, most - tallies[sink]) // 2
    margin = jnp.where((donor == sequence[0]) | (sink == sequence[0]) | (tallies[sink] == 0), 0, jnp.maximum(margin, 0))
    moved = jax.random.randint(jax.random.fold_in(own, 4), (number_of // 2,), 0, 1 << 20) % (margin + 1)
    tallies = tallies.at[donor].add(-moved).at[sink].add(moved)
    items = jnp.searchsorted(jnp.cumsum(tallies), jnp.arange(rows * top), side="right").astype(jnp.int32)
    table = items.reshape(top, rows).T
    table = table[jax.random.permutation(jax.random.fold_in(own, 1), rows)]
    rotation = jax.random.randint(jax.random.fold_in(own, 2), (rows, 1), 0, top)
    return jnp.take_along_axis(table, (jnp.arange(top)[None, :] + rotation) % top, axis=1)


def shares(amount, total, bound, slope, full):
    weights = [(1 << 20) // math.isqrt(standing ** slope) + 1 for standing in range(1, amount + 1)]
    largest = bound if full else min(bound, max(-(-total // amount), total * weights[0] // sum(weights)))
    least = 1 if total - largest >= amount - 1 else 0
    holding, rest = [largest] + [least] * (amount - 1), total - largest - least * (amount - 1)
    while rest > 0:
        candidates = [i for i in range(1, amount) if holding[i] < largest] or [i for i in range(1, amount) if holding[i] < bound]
        pool, remaining = sum([weights[i] for i in candidates]), rest
        for i in candidates:
            addition = min(bound - holding[i], max(1, remaining * weights[i] // pool), rest)
            holding[i] = holding[i] + addition
            rest = rest - addition
    return np.array(holding)


def normal_values(own_key, shape, spread, limit, pieces=(), kind=jnp.bfloat16):
    array = jax.random.normal(own_key, shape, jnp.float32) * spread
    if len(pieces) > 0:
        array = level_of(own_key, shape, pieces, -0.22, 0.18) * array
    return jnp.clip(array, min=-limit, max=limit).astype(kind)


def setup_inputs(seed: int = 0) -> dict:
    arg_keys = jax.random.split(jax.random.key(seed), 8)
    gas_fields = draw_gas_fields(jax.random.fold_in(arg_keys[7], 71), 0)
    orbit_shift = place_ends(jax.random.randint(arg_keys[1], (NR,), 0, NPHI), jax.random.fold_in(arg_keys[1], 1), 0, NPHI - 1).astype(jnp.int32)
    particle_velocity = normal_values(arg_keys[2], (3, NPART), 1.0, 6.0, ((1, 128),), jnp.float32)
    particle_mass = jnp.clip(jnp.exp(math.log(2.0) - 2.3025851 * jax.random.uniform(arg_keys[3], (NPART,), jnp.float32) ** level_of(arg_keys[3], (NPART,), ((0, 128),), -0.2, 0.2)), 0.2, 2.0)
    particle_stop = jnp.clip(jnp.exp(math.log(10.0) - 4.6051702 * jax.random.uniform(arg_keys[4], (NPART,), jnp.float32) ** level_of(arg_keys[4], (NPART,), ((0, 128),), -0.2, 0.2)), 0.1, 10.0)
    particle_cell = place_ends(jax.random.randint(arg_keys[5], (NPART,), 0, CR * ZL * CP), jax.random.fold_in(arg_keys[5], 1), 0, (CR * ZL * CP) - 1).astype(jnp.int32)
    particle_dest_keys = jax.random.split(jax.random.fold_in(arg_keys[6], 1), NPART // PD)
    particle_dest_turns = jax.random.permutation(jax.random.fold_in(arg_keys[6], 3), NPART // PD)
    particle_dest = jax.vmap(lambda own, number: routed_block(jax.random.fold_in(arg_keys[6], 2), own, number, PD, DEVICES, 1, CAP, 2))(particle_dest_keys, particle_dest_turns).reshape((NPART, 1))
    return dict(gas_fields=gas_fields, orbit_shift=orbit_shift, particle_velocity=particle_velocity, particle_mass=particle_mass, particle_stop=particle_stop, particle_cell=particle_cell, particle_dest=particle_dest)


sound_speed = 1.0
radial_rate = 0.2
azimuth_rate = 0.2


def limited_slope(left_step, right_step):
    return 0.5 * (jnp.sign(left_step) + jnp.sign(right_step)) * jnp.minimum(jnp.abs(left_step), jnp.abs(right_step))


def plm_divergence(values, speed, along_axis, extent):
    def take_range(source, offset_at, length):
        return lax.slice_in_dim(source, offset_at, offset_at + length, axis=along_axis)

    left_step = take_range(values, 1, extent + 2) - take_range(values, 0, extent + 2)
    right_step = take_range(values, 2, extent + 2) - take_range(values, 1, extent + 2)
    slopes = limited_slope(left_step, right_step)
    centre = take_range(values, 1, extent + 2)
    left_value = take_range(centre, 0, extent + 1) + 0.5 * take_range(slopes, 0, extent + 1)
    right_value = take_range(centre, 1, extent + 1) - 0.5 * take_range(slopes, 1, extent + 1)
    face_speed = 0.5 * (take_range(speed, 1, extent + 1) + take_range(speed, 2, extent + 1))
    face_flux = face_speed * 0.5 * (left_value + right_value) - 0.5 * (jnp.abs(face_speed) + sound_speed) * (right_value - left_value)
    return take_range(face_flux, 1, extent) - take_range(face_flux, 0, extent)


def reference(gas_fields, orbit_shift, particle_velocity, particle_mass, particle_stop, particle_cell, particle_dest):
    azimuth = jnp.arange(NPHI, dtype=jnp.int32)
    source_cell = (azimuth[None, :] - orbit_shift[:, None]) % NPHI
    gather_index = jnp.broadcast_to(source_cell[None, :, None, :], gas_fields.shape).astype(jnp.int32)
    shifted = jnp.take_along_axis(gas_fields, gather_index, axis=3)

    records = jnp.concatenate([particle_velocity, particle_mass[None], particle_stop[None], particle_cell[None].astype(jnp.float32)], axis=0)
    record_sets = records.reshape(6, DEVICES, PD).transpose(1, 0, 2)
    target_sets = particle_dest[:, 0].reshape(DEVICES, PD)

    def pack_outbox(pair):
        record_block, target_block = pair
        hits = (target_block[:, None] == jnp.arange(DEVICES, dtype=jnp.int32)[None, :]).astype(jnp.int32)
        slot = jnp.sum(jnp.cumsum(hits, axis=0) * hits, axis=1) - 1
        return jnp.zeros((6, DEVICES, CAP), jnp.float32).at[:, target_block, slot].set(record_block)

    outboxes = lax.map(pack_outbox, (record_sets, target_sets))
    arrived = outboxes.transpose(2, 1, 0, 3).reshape(DEVICES, 6, DEVICES * CAP)
    cells = arrived[:, 5].astype(jnp.int32)
    owner = jnp.arange(DEVICES, dtype=jnp.int32)
    row_local = cells // CP
    radius = (owner // N_SEC)[:, None] * CR + row_local // ZL
    layer = row_local % ZL
    angle_cell = (owner % N_SEC)[:, None] * CP + cells % CP
    velocity = shifted[1:4] / shifted[0:1]
    local_speed = velocity[:, radius, layer, angle_cell]
    fraction = arrived[:, 4] / (1.0 + arrived[:, 4])
    incoming = arrived[:, 0:3].transpose(1, 0, 2)
    change = (incoming - local_speed) * fraction[None]
    arrived_velocity = (incoming - change).reshape(3, DEVICES * DEVICES * CAP)
    impulse = arrived[:, 3][None] * change
    deposit = jnp.zeros((3, NR, ZL, NPHI), jnp.float32).at[:, radius, layer, angle_cell].add(impulse)
    dragged = jnp.concatenate([shifted[0:1], shifted[1:4] + deposit, shifted[4:5]], axis=0)

    radial_speed = dragged[1] / dragged[0]
    azimuthal_speed = dragged[2] / dragged[0]
    radial_pad = jnp.pad(dragged, ((0, 0), (2, 2), (0, 0), (0, 0)))
    radial_speed_pad = jnp.pad(radial_speed, ((2, 2), (0, 0), (0, 0)))
    azimuth_pad = jnp.pad(dragged, ((0, 0), (0, 0), (0, 0), (2, 2)), mode="wrap")
    azimuth_speed_pad = jnp.pad(azimuthal_speed, ((0, 0), (0, 0), (2, 2)), mode="wrap")

    def radial_field(values):
        return plm_divergence(values[None], radial_speed_pad[None], 1, NR)[0]

    def azimuth_field(values):
        return plm_divergence(values[None], azimuth_speed_pad[None], 3, NPHI)[0]

    radial_change = lax.map(radial_field, radial_pad)
    azimuth_change = lax.map(azimuth_field, azimuth_pad)
    gas_next = dragged - radial_rate * radial_change - azimuth_rate * azimuth_change
    return gas_next, arrived_velocity
```

```python
import jax
import jax.numpy as jnp
from jax import lax
from jax.sharding import PartitionSpec as P

sound_speed = 1.0
radial_rate = 0.2
azimuth_rate = 0.2
exact = lax.Precision.HIGHEST


def passed_along(block, axis, distance):
    devices = range(lax.axis_size(axis))
    route = [((i - distance) % len(devices), i) for i in devices]
    return lax.ppermute(block, axis, route)


def with_halo(cells, sides, width, closed):
    for axis, dim in sides:
        count = lax.axis_size(axis)
        ends = count if closed else count - 1
        head = lax.slice_in_dim(cells, 0, width, axis=dim)
        tail = lax.slice_in_dim(cells, cells.shape[dim] - width, cells.shape[dim], axis=dim)
        cells = jnp.concatenate(
            [
                lax.ppermute(tail, axis, [(i, (i + 1) % count) for i in range(ends)]),
                cells,
                lax.ppermute(head, axis, [((i + 1) % count, i) for i in range(ends)]),
            ],
            axis=dim,
        )
    return cells


def limited_slope(left_step, right_step):
    return (
        0.5
        * (jnp.sign(left_step) + jnp.sign(right_step))
        * jnp.minimum(jnp.abs(left_step), jnp.abs(right_step))
    )


def plm_divergence(values, speed, along_axis, extent):

    def take_range(source, offset_at, length):
        return lax.slice_in_dim(source, offset_at, offset_at + length, axis=along_axis)

    left_step = take_range(values, 1, extent + 2) - take_range(values, 0, extent + 2)
    right_step = take_range(values, 2, extent + 2) - take_range(values, 1, extent + 2)
    slopes = limited_slope(left_step, right_step)
    centre = take_range(values, 1, extent + 2)
    left_value = take_range(centre, 0, extent + 1) + 0.5 * take_range(slopes, 0, extent + 1)
    right_value = take_range(centre, 1, extent + 1) - 0.5 * take_range(slopes, 1, extent + 1)
    face_speed = 0.5 * (take_range(speed, 1, extent + 1) + take_range(speed, 2, extent + 1))
    face_flux = face_speed * 0.5 * (left_value + right_value) - 0.5 * (
        jnp.abs(face_speed) + sound_speed
    ) * (right_value - left_value)
    return take_range(face_flux, 1, extent) - take_range(face_flux, 0, extent)


def local(
    gas_fields,
    orbit_shift,
    particle_velocity,
    particle_mass,
    particle_stop,
    particle_cell,
    particle_dest,
):
    field_count, radius_count, layers, sector = gas_fields.shape
    sectors = lax.axis_size("sec")
    per_member = radius_count // sectors
    member = lax.axis_index("sec")
    ring = lax.all_to_all(gas_fields, "sec", split_axis=1, concat_axis=3, tiled=True)
    extent = ring.shape[3]
    own_shift = lax.dynamic_slice_in_dim(orbit_shift, member * per_member, per_member)
    doubled = jnp.concatenate([ring, ring], axis=3)
    rolled = jnp.concatenate(
        [
            lax.dynamic_slice_in_dim(
                doubled[:, i : i + 1], (extent - own_shift[i]) % extent, extent, axis=3
            )
            for i in range(per_member)
        ],
        axis=1,
    )
    shifted = lax.all_to_all(rolled, "sec", split_axis=3, concat_axis=1, tiled=True)
    per_device = particle_dest.shape[0]
    devices = lax.axis_size(("rad", "sec"))
    capacity = 2 * per_device // devices
    target = particle_dest[:, 0]
    hits = target[:, None] == jnp.arange(devices, dtype=jnp.int32)[None, :]
    order_index = jnp.arange(per_device, dtype=jnp.int32)
    earlier = (order_index[:, None] >= order_index[None, :]).astype(jnp.bfloat16)
    running = jnp.dot(earlier, hits.astype(jnp.bfloat16), preferred_element_type=jnp.float32)
    slot = jnp.sum(jnp.where(hits, running, 0.0), axis=1).astype(jnp.int32) - 1
    column = target * capacity + slot
    records = jnp.concatenate(
        [
            particle_velocity,
            particle_mass[None],
            particle_stop[None],
            particle_cell[None].astype(jnp.float32),
        ],
        axis=0,
    )
    block_rows = min(512, per_device)
    block_count = per_device // block_rows
    record_blocks = records.reshape(6, block_count, block_rows).transpose(1, 0, 2)
    column_blocks = column.reshape(block_count, block_rows)
    slot_ids = jnp.arange(devices * capacity, dtype=jnp.int32)

    def place_block(total, pair):
        record_block, column_block = pair
        placing = (column_block[:, None] == slot_ids[None, :]).astype(jnp.float32)
        return (
            total
            + jnp.dot(record_block, placing, precision=exact, preferred_element_type=jnp.float32),
            None,
        )

    outbox_flat, _ = lax.scan(
        place_block, jnp.zeros((6, devices * capacity), jnp.float32), (record_blocks, column_blocks)
    )
    outbox = outbox_flat.reshape(6, devices, capacity)
    inbox = lax.all_to_all(outbox, ("rad", "sec"), split_axis=1, concat_axis=1, tiled=True)
    received = inbox.reshape(6, devices * capacity)
    row_count = radius_count * layers
    velocity_rows = (
        (shifted[1:4] / shifted[0:1])
        .reshape(3, row_count, sector)
        .transpose(1, 0, 2)
        .reshape(row_count, 3 * sector)
    )
    cells = received[5].astype(jnp.int32)
    row_hot = (
        (cells // sector)[:, None] == jnp.arange(row_count, dtype=jnp.int32)[None, :]
    ).astype(jnp.float32)
    azimuth_hot = (
        (cells % sector)[:, None] == jnp.arange(sector, dtype=jnp.int32)[None, :]
    ).astype(jnp.float32)
    picked = jnp.dot(
        row_hot, velocity_rows, precision=exact, preferred_element_type=jnp.float32
    ).reshape(-1, 3, sector)
    local_speed = jnp.sum(picked * azimuth_hot[:, None, :], axis=2).T
    velocity_in = received[0:3]
    fraction = received[4] / (1.0 + received[4])
    change = (velocity_in - local_speed) * fraction[None]
    arrived_velocity = velocity_in - change
    impulse = received[3][None] * change
    spread = (impulse.T[:, :, None] * azimuth_hot[:, None, :]).reshape(-1, 3 * sector)
    deposit_rows = jnp.dot(row_hot.T, spread, precision=exact, preferred_element_type=jnp.float32)
    momentum_added = (
        deposit_rows.reshape(row_count, 3, sector)
        .transpose(1, 0, 2)
        .reshape(3, radius_count, layers, sector)
    )
    dragged = jnp.concatenate([shifted[0:1], shifted[1:4] + momentum_added, shifted[4:5]], axis=0)
    radial_speed = dragged[1] / dragged[0]
    azimuthal_speed = dragged[2] / dragged[0]
    stacked = jnp.concatenate([dragged, radial_speed[None], azimuthal_speed[None]], axis=0)
    radial_pad = with_halo(stacked, (("rad", 1),), 2, False)
    azimuth_pad = with_halo(stacked, (("sec", 3),), 2, True)
    radial_change = plm_divergence(radial_pad[0:5], radial_pad[5:6], 1, radius_count)
    azimuth_change = plm_divergence(azimuth_pad[0:5], azimuth_pad[6:7], 3, sector)
    gas_next = dragged - radial_rate * radial_change - azimuth_rate * azimuth_change
    return (gas_next, arrived_velocity)


def solution(mesh):
    placed = (
        P(None, "rad", None, "sec"),
        P("rad"),
        P(None, ("rad", "sec")),
        P(("rad", "sec")),
        P(("rad", "sec")),
        P(("rad", "sec")),
        P(("rad", "sec"), None),
    )
    return jax.shard_map(
        local,
        mesh=mesh,
        in_specs=placed,
        out_specs=(P(None, "rad", None, "sec"), P(None, ("rad", "sec"))),
        check_vma=False,
    )
```

```python
import jax
import jax.numpy as jnp
from jax import lax
from jax.sharding import PartitionSpec as P

sound_speed = 1.0
radial_rate = 0.2
azimuth_rate = 0.2
exact = lax.Precision.HIGHEST


def passed_along(block, axis, distance):
    devices = range(lax.axis_size(axis))
    route = [((i - distance) % len(devices), i) for i in devices]
    return lax.ppermute(block, axis, route)


def with_halo(cells, sides, width, closed):
    for axis, dim in sides:
        count = lax.axis_size(axis)
        ends = count if closed else count - 1
        head = lax.slice_in_dim(cells, 0, width, axis=dim)
        tail = lax.slice_in_dim(cells, cells.shape[dim] - width, cells.shape[dim], axis=dim)
        cells = jnp.concatenate(
            [
                lax.ppermute(tail, axis, [(i, (i + 1) % count) for i in range(ends)]),
                cells,
                lax.ppermute(head, axis, [((i + 1) % count, i) for i in range(ends)]),
            ],
            axis=dim,
        )
    return cells


def limited_slope(left_step, right_step):
    return (
        0.5
        * (jnp.sign(left_step) + jnp.sign(right_step))
        * jnp.minimum(jnp.abs(left_step), jnp.abs(right_step))
    )


def plm_divergence(values, speed, along_axis, extent):

    def take_range(source, offset_at, length):
        return lax.slice_in_dim(source, offset_at, offset_at + length, axis=along_axis)

    left_step = take_range(values, 1, extent + 2) - take_range(values, 0, extent + 2)
    right_step = take_range(values, 2, extent + 2) - take_range(values, 1, extent + 2)
    slopes = limited_slope(left_step, right_step)
    centre = take_range(values, 1, extent + 2)
    left_value = take_range(centre, 0, extent + 1) + 0.5 * take_range(slopes, 0, extent + 1)
    right_value = take_range(centre, 1, extent + 1) - 0.5 * take_range(slopes, 1, extent + 1)
    face_speed = 0.5 * (take_range(speed, 1, extent + 1) + take_range(speed, 2, extent + 1))
    face_flux = face_speed * 0.5 * (left_value + right_value) - 0.5 * (
        jnp.abs(face_speed) + sound_speed
    ) * (right_value - left_value)
    return take_range(face_flux, 1, extent) - take_range(face_flux, 0, extent)


def local(
    gas_fields,
    orbit_shift,
    particle_velocity,
    particle_mass,
    particle_stop,
    particle_cell,
    particle_dest,
):
    field_count, radius_count, layers, sector = gas_fields.shape
    sectors = lax.axis_size("sec")
    per_member = radius_count // sectors
    member = lax.axis_index("sec")
    by_radius = gas_fields.transpose(1, 0, 2, 3)
    ring = lax.all_to_all(by_radius, "sec", split_axis=0, concat_axis=0, tiled=True)
    ring = ring.reshape(sectors, per_member, field_count, layers, sector)
    own_shift = lax.dynamic_slice_in_dim(orbit_shift, member * per_member, per_member)
    rolled = []
    for i in range(per_member):
        quotient = own_shift[i] // sector
        remainder = own_shift[i] % sector
        doubled = jnp.concatenate([ring[:, i], ring[:, i]], axis=0)
        current = lax.dynamic_slice_in_dim(doubled, (sectors - quotient) % sectors, sectors, axis=0)
        preceding = lax.dynamic_slice_in_dim(
            doubled, (sectors - quotient - 1) % sectors, sectors, axis=0
        )
        window = jnp.concatenate([preceding, current], axis=3)
        for bit_level in range((sector - 1).bit_length()):
            step_size = 1 << bit_level
            moved = jnp.concatenate(
                [
                    jnp.zeros(window.shape[:3] + (step_size,), jnp.float32),
                    window[..., :-step_size],
                ],
                axis=3,
            )
            window = jnp.where(remainder >> bit_level & 1 == 1, moved, window)
        rolled.append(window[..., sector:])
    rolled = jnp.stack(rolled, axis=1).reshape(sectors * per_member, field_count, layers, sector)
    shifted = lax.all_to_all(rolled, "sec", split_axis=0, concat_axis=0, tiled=True)
    shifted = shifted.transpose(1, 0, 2, 3)
    per_device = particle_dest.shape[0]
    devices = lax.axis_size(("rad", "sec"))
    capacity = 2 * per_device // devices
    target = particle_dest[:, 0]
    hits = target[:, None] == jnp.arange(devices, dtype=jnp.int32)[None, :]
    order_index = jnp.arange(per_device, dtype=jnp.int32)
    earlier = (order_index[:, None] >= order_index[None, :]).astype(jnp.bfloat16)
    running = jnp.dot(earlier, hits.astype(jnp.bfloat16), preferred_element_type=jnp.float32)
    slot = jnp.sum(jnp.where(hits, running, 0.0), axis=1).astype(jnp.int32) - 1
    column = target * capacity + slot
    records = jnp.concatenate(
        [
            particle_velocity,
            particle_mass[None],
            particle_stop[None],
            particle_cell[None].astype(jnp.float32),
        ],
        axis=0,
    )
    block_rows = min(512, per_device)
    block_count = per_device // block_rows
    record_blocks = records.reshape(6, block_count, block_rows).transpose(1, 0, 2)
    column_blocks = column.reshape(block_count, block_rows)
    slot_ids = jnp.arange(devices * capacity, dtype=jnp.int32)

    def place_block(total, pair):
        record_block, column_block = pair
        placing = (column_block[:, None] == slot_ids[None, :]).astype(jnp.float32)
        return (
            total
            + jnp.dot(record_block, placing, precision=exact, preferred_element_type=jnp.float32),
            None,
        )

    outbox_flat, _ = lax.scan(
        place_block, jnp.zeros((6, devices * capacity), jnp.float32), (record_blocks, column_blocks)
    )
    outbox = outbox_flat.reshape(6, devices, capacity)
    inbox = lax.all_to_all(outbox, ("rad", "sec"), split_axis=1, concat_axis=1, tiled=True)
    received = inbox.reshape(6, devices * capacity)
    row_count = radius_count * layers
    velocity_rows = (
        (shifted[1:4] / shifted[0:1])
        .reshape(3, row_count, sector)
        .transpose(1, 0, 2)
        .reshape(row_count, 3 * sector)
    )
    cells = received[5].astype(jnp.int32)
    row_hot = (
        (cells // sector)[:, None] == jnp.arange(row_count, dtype=jnp.int32)[None, :]
    ).astype(jnp.float32)
    azimuth_hot = (
        (cells % sector)[:, None] == jnp.arange(sector, dtype=jnp.int32)[None, :]
    ).astype(jnp.float32)
    picked = jnp.dot(
        row_hot, velocity_rows, precision=exact, preferred_element_type=jnp.float32
    ).reshape(-1, 3, sector)
    local_speed = jnp.sum(picked * azimuth_hot[:, None, :], axis=2).T
    velocity_in = received[0:3]
    fraction = received[4] / (1.0 + received[4])
    change = (velocity_in - local_speed) * fraction[None]
    arrived_velocity = velocity_in - change
    impulse = received[3][None] * change
    spread = (impulse.T[:, :, None] * azimuth_hot[:, None, :]).reshape(-1, 3 * sector)
    deposit_rows = jnp.dot(row_hot.T, spread, precision=exact, preferred_element_type=jnp.float32)
    momentum_added = (
        deposit_rows.reshape(row_count, 3, sector)
        .transpose(1, 0, 2)
        .reshape(3, radius_count, layers, sector)
    )
    dragged = jnp.concatenate([shifted[0:1], shifted[1:4] + momentum_added, shifted[4:5]], axis=0)
    radial_speed = dragged[1] / dragged[0]
    azimuthal_speed = dragged[2] / dragged[0]
    stacked = jnp.concatenate([dragged, radial_speed[None], azimuthal_speed[None]], axis=0)
    radial_pad = with_halo(stacked, (("rad", 1),), 2, False)
    azimuth_pad = with_halo(stacked, (("sec", 3),), 2, True)
    radial_change = plm_divergence(radial_pad[0:5], radial_pad[5:6], 1, radius_count)
    azimuth_change = plm_divergence(azimuth_pad[0:5], azimuth_pad[6:7], 3, sector)
    gas_next = dragged - radial_rate * radial_change - azimuth_rate * azimuth_change
    return (gas_next, arrived_velocity)


def solution(mesh):
    placed = (
        P(None, "rad", None, "sec"),
        P("rad"),
        P(None, ("rad", "sec")),
        P(("rad", "sec")),
        P(("rad", "sec")),
        P(("rad", "sec")),
        P(("rad", "sec"), None),
    )
    return jax.shard_map(
        local,
        mesh=mesh,
        in_specs=placed,
        out_specs=(P(None, "rad", None, "sec"), P(None, ("rad", "sec"))),
        check_vma=False,
    )
```

```python
import jax
import jax.numpy as jnp
from jax import lax
from jax.sharding import PartitionSpec as P

sound_speed = 1.0
radial_rate = 0.2
azimuth_rate = 0.2
exact = lax.Precision.HIGHEST


def passed_along(block, axis, distance):
    devices = range(lax.axis_size(axis))
    route = [((i - distance) % len(devices), i) for i in devices]
    return lax.ppermute(block, axis, route)


def with_halo(cells, sides, width, closed):
    for axis, dim in sides:
        count = lax.axis_size(axis)
        ends = count if closed else count - 1
        head = lax.slice_in_dim(cells, 0, width, axis=dim)
        tail = lax.slice_in_dim(cells, cells.shape[dim] - width, cells.shape[dim], axis=dim)
        cells = jnp.concatenate(
            [
                lax.ppermute(tail, axis, [(i, (i + 1) % count) for i in range(ends)]),
                cells,
                lax.ppermute(head, axis, [((i + 1) % count, i) for i in range(ends)]),
            ],
            axis=dim,
        )
    return cells


def limited_slope(left_step, right_step):
    return (
        0.5
        * (jnp.sign(left_step) + jnp.sign(right_step))
        * jnp.minimum(jnp.abs(left_step), jnp.abs(right_step))
    )


def plm_divergence(values, speed, along_axis, extent):

    def take_range(source, offset_at, length):
        return lax.slice_in_dim(source, offset_at, offset_at + length, axis=along_axis)

    left_step = take_range(values, 1, extent + 2) - take_range(values, 0, extent + 2)
    right_step = take_range(values, 2, extent + 2) - take_range(values, 1, extent + 2)
    slopes = limited_slope(left_step, right_step)
    centre = take_range(values, 1, extent + 2)
    left_value = take_range(centre, 0, extent + 1) + 0.5 * take_range(slopes, 0, extent + 1)
    right_value = take_range(centre, 1, extent + 1) - 0.5 * take_range(slopes, 1, extent + 1)
    face_speed = 0.5 * (take_range(speed, 1, extent + 1) + take_range(speed, 2, extent + 1))
    face_flux = face_speed * 0.5 * (left_value + right_value) - 0.5 * (
        jnp.abs(face_speed) + sound_speed
    ) * (right_value - left_value)
    return take_range(face_flux, 1, extent) - take_range(face_flux, 0, extent)


def local(
    gas_fields,
    orbit_shift,
    particle_velocity,
    particle_mass,
    particle_stop,
    particle_cell,
    particle_dest,
):
    field_count, radius_count, layers, sector = gas_fields.shape
    sectors = lax.axis_size("sec")
    per_member = radius_count // sectors
    member = lax.axis_index("sec")
    by_radius = gas_fields.transpose(1, 0, 2, 3)
    ring = lax.all_to_all(by_radius, "sec", split_axis=0, concat_axis=0, tiled=True)
    ring = ring.reshape(sectors, per_member, field_count, layers, sector)
    own_shift = lax.dynamic_slice_in_dim(orbit_shift, member * per_member, per_member)
    rolled = []
    for i in range(per_member):
        quotient = own_shift[i] // sector
        remainder = own_shift[i] % sector
        doubled = jnp.concatenate([ring[:, i], ring[:, i]], axis=0)
        current = lax.dynamic_slice_in_dim(doubled, (sectors - quotient) % sectors, sectors, axis=0)
        preceding = lax.dynamic_slice_in_dim(
            doubled, (sectors - quotient - 1) % sectors, sectors, axis=0
        )
        window = jnp.concatenate([preceding, current], axis=3)
        for bit_level in range((sector - 1).bit_length()):
            step_size = 1 << bit_level
            moved = jnp.concatenate(
                [
                    jnp.zeros(window.shape[:3] + (step_size,), jnp.float32),
                    window[..., :-step_size],
                ],
                axis=3,
            )
            window = jnp.where(remainder >> bit_level & 1 == 1, moved, window)
        rolled.append(window[..., sector:])
    rolled = jnp.stack(rolled, axis=1).reshape(sectors * per_member, field_count, layers, sector)
    shifted = lax.all_to_all(rolled, "sec", split_axis=0, concat_axis=0, tiled=True)
    shifted = shifted.transpose(1, 0, 2, 3)
    per_device = particle_dest.shape[0]
    devices = lax.axis_size(("rad", "sec"))
    capacity = 2 * per_device // devices
    target = particle_dest[:, 0]
    hits = target[:, None] == jnp.arange(devices, dtype=jnp.int32)[None, :]
    block_rows = min(128, per_device)
    block_count = per_device // block_rows
    hit_blocks = hits.astype(jnp.bfloat16).reshape(block_count, block_rows, devices)
    row_index = jnp.arange(block_rows, dtype=jnp.int32)
    within = (row_index[:, None] >= row_index[None, :]).astype(jnp.bfloat16)
    block_index = jnp.arange(block_count, dtype=jnp.int32)
    before = (block_index[:, None] > block_index[None, :]).astype(jnp.bfloat16)
    block_totals = jnp.sum(hit_blocks, axis=1, dtype=jnp.float32).astype(jnp.bfloat16)
    running = jnp.einsum(
        "ij,bjd->bid", within, hit_blocks, preferred_element_type=jnp.float32
    ) + jnp.dot(before, block_totals, preferred_element_type=jnp.float32)[:, None, :]
    running = running.reshape(per_device, devices)
    slot = jnp.sum(jnp.where(hits, running, 0.0), axis=1).astype(jnp.int32) - 1
    records = jnp.concatenate(
        [
            particle_velocity,
            particle_mass[None],
            particle_stop[None],
            particle_cell[None].astype(jnp.float32),
        ],
        axis=0,
    )
    slot_hot = slot[:, None] == jnp.arange(capacity, dtype=jnp.int32)[None, :]
    spread_records = jnp.where(slot_hot[:, None, :], records.T[:, :, None], 0.0).reshape(
        per_device, 6 * capacity
    )
    outbox = jnp.dot(
        hits.astype(jnp.float32).T, spread_records, precision=exact, preferred_element_type=jnp.float32
    ).reshape(devices, 6, capacity)
    inbox = lax.all_to_all(outbox, ("rad", "sec"), split_axis=0, concat_axis=0, tiled=True)
    received = inbox.transpose(1, 0, 2).reshape(6, devices * capacity)
    row_count = radius_count * layers
    velocity_rows = (
        (shifted[1:4] / shifted[0:1])
        .reshape(3, row_count, sector)
        .transpose(1, 0, 2)
        .reshape(row_count, 3 * sector)
    )
    cells = received[5].astype(jnp.int32)
    row_hot = (
        (cells // sector)[:, None] == jnp.arange(row_count, dtype=jnp.int32)[None, :]
    ).astype(jnp.float32)
    azimuth_hot = (
        (cells % sector)[:, None] == jnp.arange(sector, dtype=jnp.int32)[None, :]
    ).astype(jnp.float32)
    picked = jnp.dot(
        row_hot, velocity_rows, precision=exact, preferred_element_type=jnp.float32
    ).reshape(-1, 3, sector)
    local_speed = jnp.sum(picked * azimuth_hot[:, None, :], axis=2).T
    velocity_in = received[0:3]
    fraction = received[4] / (1.0 + received[4])
    change = (velocity_in - local_speed) * fraction[None]
    arrived_velocity = velocity_in - change
    impulse = received[3][None] * change
    spread = (impulse.T[:, :, None] * azimuth_hot[:, None, :]).reshape(-1, 3 * sector)
    deposit_rows = jnp.dot(row_hot.T, spread, precision=exact, preferred_element_type=jnp.float32)
    momentum_added = (
        deposit_rows.reshape(row_count, 3, sector)
        .transpose(1, 0, 2)
        .reshape(3, radius_count, layers, sector)
    )
    dragged = jnp.concatenate([shifted[0:1], shifted[1:4] + momentum_added, shifted[4:5]], axis=0)
    radial_speed = dragged[1] / dragged[0]
    azimuthal_speed = dragged[2] / dragged[0]
    stacked = jnp.concatenate([dragged, radial_speed[None], azimuthal_speed[None]], axis=0)
    radial_pad = with_halo(stacked, (("rad", 1),), 2, False)
    azimuth_pad = with_halo(stacked, (("sec", 3),), 2, True)
    radial_change = plm_divergence(radial_pad[0:5], radial_pad[5:6], 1, radius_count)
    azimuth_change = plm_divergence(azimuth_pad[0:5], azimuth_pad[6:7], 3, sector)
    gas_next = dragged - radial_rate * radial_change - azimuth_rate * azimuth_change
    return (gas_next, arrived_velocity)


def solution(mesh):
    placed = (
        P(None, "rad", None, "sec"),
        P("rad"),
        P(None, ("rad", "sec")),
        P(("rad", "sec")),
        P(("rad", "sec")),
        P(("rad", "sec")),
        P(("rad", "sec"), None),
    )
    return jax.shard_map(
        local,
        mesh=mesh,
        in_specs=placed,
        out_specs=(P(None, "rad", None, "sec"), P(None, ("rad", "sec"))),
        check_vma=False,
    )
```

```python
import jax
import jax.numpy as jnp
from jax import lax
from jax.sharding import PartitionSpec as P

sound_speed = 1.0
radial_rate = 0.2
azimuth_rate = 0.2
exact = lax.Precision.HIGHEST


def passed_along(block, axis, distance):
    devices = range(lax.axis_size(axis))
    route = [((i - distance) % len(devices), i) for i in devices]
    return lax.ppermute(block, axis, route)


def with_halo(cells, sides, width, closed):
    for axis, dim in sides:
        count = lax.axis_size(axis)
        ends = count if closed else count - 1
        head = lax.slice_in_dim(cells, 0, width, axis=dim)
        tail = lax.slice_in_dim(cells, cells.shape[dim] - width, cells.shape[dim], axis=dim)
        cells = jnp.concatenate(
            [
                lax.ppermute(tail, axis, [(i, (i + 1) % count) for i in range(ends)]),
                cells,
                lax.ppermute(head, axis, [((i + 1) % count, i) for i in range(ends)]),
            ],
            axis=dim,
        )
    return cells


def limited_slope(left_step, right_step):
    return (
        0.5
        * (jnp.sign(left_step) + jnp.sign(right_step))
        * jnp.minimum(jnp.abs(left_step), jnp.abs(right_step))
    )


def plm_divergence(values, speed, along_axis, extent):

    def take_range(source, offset_at, length):
        return lax.slice_in_dim(source, offset_at, offset_at + length, axis=along_axis)

    left_step = take_range(values, 1, extent + 2) - take_range(values, 0, extent + 2)
    right_step = take_range(values, 2, extent + 2) - take_range(values, 1, extent + 2)
    slopes = limited_slope(left_step, right_step)
    centre = take_range(values, 1, extent + 2)
    left_value = take_range(centre, 0, extent + 1) + 0.5 * take_range(slopes, 0, extent + 1)
    right_value = take_range(centre, 1, extent + 1) - 0.5 * take_range(slopes, 1, extent + 1)
    face_speed = 0.5 * (take_range(speed, 1, extent + 1) + take_range(speed, 2, extent + 1))
    face_flux = face_speed * 0.5 * (left_value + right_value) - 0.5 * (
        jnp.abs(face_speed) + sound_speed
    ) * (right_value - left_value)
    return take_range(face_flux, 1, extent) - take_range(face_flux, 0, extent)


def local(
    gas_fields,
    orbit_shift,
    particle_velocity,
    particle_mass,
    particle_stop,
    particle_cell,
    particle_dest,
):
    field_count, radius_count, layers, sector = gas_fields.shape
    sectors = lax.axis_size("sec")
    per_member = radius_count // sectors
    member = lax.axis_index("sec")
    by_radius = gas_fields.transpose(1, 0, 2, 3)
    ring = lax.all_to_all(by_radius, "sec", split_axis=0, concat_axis=0, tiled=True)
    ring = ring.reshape(sectors, per_member, field_count, layers, sector)
    own_shift = lax.dynamic_slice_in_dim(orbit_shift, member * per_member, per_member)
    rolled = []
    for i in range(per_member):
        quotient = own_shift[i] // sector
        remainder = own_shift[i] % sector
        doubled = jnp.concatenate([ring[:, i], ring[:, i]], axis=0)
        current = lax.dynamic_slice_in_dim(doubled, (sectors - quotient) % sectors, sectors, axis=0)
        preceding = lax.dynamic_slice_in_dim(
            doubled, (sectors - quotient - 1) % sectors, sectors, axis=0
        )
        window = jnp.concatenate([preceding, current], axis=3)
        for bit_level in range((sector - 1).bit_length()):
            step_size = 1 << bit_level
            moved = jnp.concatenate(
                [
                    jnp.zeros(window.shape[:3] + (step_size,), jnp.float32),
                    window[..., :-step_size],
                ],
                axis=3,
            )
            window = jnp.where(remainder >> bit_level & 1 == 1, moved, window)
        rolled.append(window[..., sector:])
    rolled = jnp.stack(rolled, axis=1).reshape(sectors * per_member, field_count, layers, sector)
    shifted = lax.all_to_all(rolled, "sec", split_axis=0, concat_axis=0, tiled=True)
    shifted = shifted.transpose(1, 0, 2, 3)
    per_device = particle_dest.shape[0]
    devices = lax.axis_size(("rad", "sec"))
    capacity = 2 * per_device // devices
    target = particle_dest[:, 0]
    hits = target[:, None] == jnp.arange(devices, dtype=jnp.int32)[None, :]
    block_rows = min(128, per_device)
    block_count = per_device // block_rows
    hit_blocks = hits.astype(jnp.bfloat16).reshape(block_count, block_rows, devices)
    row_index = jnp.arange(block_rows, dtype=jnp.int32)
    within = (row_index[:, None] >= row_index[None, :]).astype(jnp.bfloat16)
    block_index = jnp.arange(block_count, dtype=jnp.int32)
    before = (block_index[:, None] > block_index[None, :]).astype(jnp.bfloat16)
    block_totals = jnp.sum(hit_blocks, axis=1, dtype=jnp.float32).astype(jnp.bfloat16)
    running = jnp.einsum(
        "ij,bjd->bid", within, hit_blocks, preferred_element_type=jnp.float32
    ) + jnp.dot(before, block_totals, preferred_element_type=jnp.float32)[:, None, :]
    running = running.reshape(per_device, devices)
    slot = jnp.sum(jnp.where(hits, running, 0.0), axis=1).astype(jnp.int32) - 1
    records = jnp.concatenate(
        [
            particle_velocity,
            particle_mass[None],
            particle_stop[None],
            particle_cell[None].astype(jnp.float32),
        ],
        axis=0,
    )
    slot_hot = slot[:, None] == jnp.arange(capacity, dtype=jnp.int32)[None, :]
    spread_records = jnp.where(slot_hot[:, None, :], records.T[:, :, None], 0.0).reshape(
        per_device, 6 * capacity
    )
    outbox = jnp.dot(
        hits.astype(jnp.float32).T, spread_records, precision=exact, preferred_element_type=jnp.float32
    ).reshape(devices, 6, capacity)
    inbox = lax.all_to_all(outbox, ("rad", "sec"), split_axis=0, concat_axis=0, tiled=True)
    received = inbox.transpose(1, 0, 2).reshape(6, devices * capacity)
    row_count = radius_count * layers
    velocity_table = (shifted[1:4] / shifted[0:1]).reshape(3, row_count * sector)
    cells = received[5].astype(jnp.int32)
    local_speed = jnp.stack(
        [jnp.take(velocity_table[k], cells, mode="clip") for k in range(3)], axis=0
    )
    velocity_in = received[0:3]
    fraction = received[4] / (1.0 + received[4])
    change = (velocity_in - local_speed) * fraction[None]
    arrived_velocity = velocity_in - change
    impulse = received[3][None] * change
    momentum_added = jnp.stack(
        [
            jnp.zeros((row_count * sector,), jnp.float32).at[cells].add(impulse[k], mode="drop")
            for k in range(3)
        ],
        axis=0,
    ).reshape(3, radius_count, layers, sector)
    dragged = jnp.concatenate([shifted[0:1], shifted[1:4] + momentum_added, shifted[4:5]], axis=0)
    radial_speed = dragged[1] / dragged[0]
    azimuthal_speed = dragged[2] / dragged[0]
    stacked = jnp.concatenate([dragged, radial_speed[None], azimuthal_speed[None]], axis=0)
    radial_pad = with_halo(stacked, (("rad", 1),), 2, False)
    azimuth_pad = with_halo(stacked, (("sec", 3),), 2, True)
    radial_change = plm_divergence(radial_pad[0:5], radial_pad[5:6], 1, radius_count)
    azimuth_change = plm_divergence(azimuth_pad[0:5], azimuth_pad[6:7], 3, sector)
    gas_next = dragged - radial_rate * radial_change - azimuth_rate * azimuth_change
    return (gas_next, arrived_velocity)


def solution(mesh):
    placed = (
        P(None, "rad", None, "sec"),
        P("rad"),
        P(None, ("rad", "sec")),
        P(("rad", "sec")),
        P(("rad", "sec")),
        P(("rad", "sec")),
        P(("rad", "sec"), None),
    )
    return jax.shard_map(
        local,
        mesh=mesh,
        in_specs=placed,
        out_specs=(P(None, "rad", None, "sec"), P(None, ("rad", "sec"))),
        check_vma=False,
    )
```

```python
import jax
import jax.numpy as jnp
from jax import lax
from jax.sharding import PartitionSpec as P

sound_speed = 1.0
radial_rate = 0.2
azimuth_rate = 0.2
exact = lax.Precision.HIGHEST


def passed_along(block, axis, distance):
    devices = range(lax.axis_size(axis))
    route = [((i - distance) % len(devices), i) for i in devices]
    return lax.ppermute(block, axis, route)


def with_halo(cells, sides, width, closed):
    for axis, dim in sides:
        count = lax.axis_size(axis)
        ends = count if closed else count - 1
        head = lax.slice_in_dim(cells, 0, width, axis=dim)
        tail = lax.slice_in_dim(cells, cells.shape[dim] - width, cells.shape[dim], axis=dim)
        cells = jnp.concatenate(
            [
                lax.ppermute(tail, axis, [(i, (i + 1) % count) for i in range(ends)]),
                cells,
                lax.ppermute(head, axis, [((i + 1) % count, i) for i in range(ends)]),
            ],
            axis=dim,
        )
    return cells


def limited_slope(left_step, right_step):
    return (
        0.5
        * (jnp.sign(left_step) + jnp.sign(right_step))
        * jnp.minimum(jnp.abs(left_step), jnp.abs(right_step))
    )


def plm_divergence(values, speed, along_axis, extent):

    def take_range(source, offset_at, length):
        return lax.slice_in_dim(source, offset_at, offset_at + length, axis=along_axis)

    left_step = take_range(values, 1, extent + 2) - take_range(values, 0, extent + 2)
    right_step = take_range(values, 2, extent + 2) - take_range(values, 1, extent + 2)
    slopes = limited_slope(left_step, right_step)
    centre = take_range(values, 1, extent + 2)
    left_value = take_range(centre, 0, extent + 1) + 0.5 * take_range(slopes, 0, extent + 1)
    right_value = take_range(centre, 1, extent + 1) - 0.5 * take_range(slopes, 1, extent + 1)
    face_speed = 0.5 * (take_range(speed, 1, extent + 1) + take_range(speed, 2, extent + 1))
    face_flux = face_speed * 0.5 * (left_value + right_value) - 0.5 * (
        jnp.abs(face_speed) + sound_speed
    ) * (right_value - left_value)
    return take_range(face_flux, 1, extent) - take_range(face_flux, 0, extent)


def local(
    gas_fields,
    orbit_shift,
    particle_velocity,
    particle_mass,
    particle_stop,
    particle_cell,
    particle_dest,
):
    field_count, radius_count, layers, sector = gas_fields.shape
    sectors = lax.axis_size("sec")
    per_member = radius_count // sectors
    member = lax.axis_index("sec")
    by_radius = gas_fields.transpose(1, 0, 2, 3)
    ring = lax.all_to_all(by_radius, "sec", split_axis=0, concat_axis=0, tiled=True)
    ring = ring.reshape(sectors, per_member, field_count, layers, sector)
    own_shift = lax.dynamic_slice_in_dim(orbit_shift, member * per_member, per_member)
    rolled = []
    for i in range(per_member):
        quotient = own_shift[i] // sector
        remainder = own_shift[i] % sector
        doubled = jnp.concatenate([ring[:, i], ring[:, i]], axis=0)
        current = lax.dynamic_slice_in_dim(doubled, (sectors - quotient) % sectors, sectors, axis=0)
        preceding = lax.dynamic_slice_in_dim(
            doubled, (sectors - quotient - 1) % sectors, sectors, axis=0
        )
        window = jnp.concatenate([preceding, current], axis=3)
        for bit_level in range((sector - 1).bit_length()):
            step_size = 1 << bit_level
            moved = jnp.concatenate(
                [
                    jnp.zeros(window.shape[:3] + (step_size,), jnp.float32),
                    window[..., :-step_size],
                ],
                axis=3,
            )
            window = jnp.where(remainder >> bit_level & 1 == 1, moved, window)
        rolled.append(window[..., sector:])
    rolled = jnp.stack(rolled, axis=1).reshape(sectors * per_member, field_count, layers, sector)
    shifted = lax.all_to_all(rolled, "sec", split_axis=0, concat_axis=0, tiled=True)
    shifted = shifted.transpose(1, 0, 2, 3)
    per_device = particle_dest.shape[0]
    devices = lax.axis_size(("rad", "sec"))
    capacity = 2 * per_device // devices
    target = particle_dest[:, 0]
    hits = target[:, None] == jnp.arange(devices, dtype=jnp.int32)[None, :]
    block_rows = min(128, per_device)
    block_count = per_device // block_rows
    hit_blocks = hits.astype(jnp.bfloat16).reshape(block_count, block_rows, devices)
    row_index = jnp.arange(block_rows, dtype=jnp.int32)
    within = (row_index[:, None] >= row_index[None, :]).astype(jnp.bfloat16)
    block_index = jnp.arange(block_count, dtype=jnp.int32)
    before = (block_index[:, None] > block_index[None, :]).astype(jnp.bfloat16)
    block_totals = jnp.sum(hit_blocks, axis=1, dtype=jnp.float32).astype(jnp.bfloat16)
    running = jnp.einsum(
        "ij,bjd->bid", within, hit_blocks, preferred_element_type=jnp.float32
    ) + jnp.dot(before, block_totals, preferred_element_type=jnp.float32)[:, None, :]
    running = running.reshape(per_device, devices)
    slot = jnp.sum(jnp.where(hits, running, 0.0), axis=1).astype(jnp.int32) - 1
    records = jnp.concatenate(
        [
            particle_velocity,
            particle_mass[None],
            particle_stop[None],
            particle_cell[None].astype(jnp.float32),
        ],
        axis=0,
    )
    slot_hot = slot[:, None] == jnp.arange(capacity, dtype=jnp.int32)[None, :]
    spread_records = jnp.where(slot_hot[:, None, :], records.T[:, :, None], 0.0).reshape(
        per_device, 6 * capacity
    )
    outbox = jnp.dot(
        hits.astype(jnp.float32).T, spread_records, precision=exact, preferred_element_type=jnp.float32
    ).reshape(devices, 6, capacity)
    inbox = lax.all_to_all(outbox, ("rad", "sec"), split_axis=0, concat_axis=0, tiled=True)
    received = inbox.transpose(1, 0, 2).reshape(6, devices * capacity)
    row_count = radius_count * layers
    velocity_rows = (
        (shifted[1:4] / shifted[0:1])
        .reshape(3, row_count, sector)
        .transpose(1, 0, 2)
        .reshape(row_count, 3 * sector)
    )
    cells = received[5].astype(jnp.int32)
    row_hot = (
        (cells // sector)[:, None] == jnp.arange(row_count, dtype=jnp.int32)[None, :]
    ).astype(jnp.float32)
    azimuth_hot = (
        (cells % sector)[:, None] == jnp.arange(sector, dtype=jnp.int32)[None, :]
    ).astype(jnp.float32)
    picked = jnp.dot(
        row_hot, velocity_rows, precision=lax.Precision.HIGH, preferred_element_type=jnp.float32
    ).reshape(-1, 3, sector)
    local_speed = jnp.sum(picked * azimuth_hot[:, None, :], axis=2).T
    velocity_in = received[0:3]
    fraction = received[4] / (1.0 + received[4])
    change = (velocity_in - local_speed) * fraction[None]
    arrived_velocity = velocity_in - change
    impulse = received[3][None] * change
    spread = (impulse.T[:, :, None] * azimuth_hot[:, None, :]).reshape(-1, 3 * sector)
    deposit_rows = jnp.dot(row_hot.T, spread, precision=lax.Precision.HIGH, preferred_element_type=jnp.float32)
    momentum_added = (
        deposit_rows.reshape(row_count, 3, sector)
        .transpose(1, 0, 2)
        .reshape(3, radius_count, layers, sector)
    )
    dragged = jnp.concatenate([shifted[0:1], shifted[1:4] + momentum_added, shifted[4:5]], axis=0)
    radial_speed = dragged[1] / dragged[0]
    azimuthal_speed = dragged[2] / dragged[0]
    stacked = jnp.concatenate([dragged, radial_speed[None], azimuthal_speed[None]], axis=0)
    radial_pad = with_halo(stacked, (("rad", 1),), 2, False)
    azimuth_pad = with_halo(stacked, (("sec", 3),), 2, True)
    radial_change = plm_divergence(radial_pad[0:5], radial_pad[5:6], 1, radius_count)
    azimuth_change = plm_divergence(azimuth_pad[0:5], azimuth_pad[6:7], 3, sector)
    gas_next = dragged - radial_rate * radial_change - azimuth_rate * azimuth_change
    return (gas_next, arrived_velocity)


def solution(mesh):
    placed = (
        P(None, "rad", None, "sec"),
        P("rad"),
        P(None, ("rad", "sec")),
        P(("rad", "sec")),
        P(("rad", "sec")),
        P(("rad", "sec")),
        P(("rad", "sec"), None),
    )
    return jax.shard_map(
        local,
        mesh=mesh,
        in_specs=placed,
        out_specs=(P(None, "rad", None, "sec"), P(None, ("rad", "sec"))),
        check_vma=False,
    )
```

```python
import jax
import jax.numpy as jnp
from jax import lax
from jax.sharding import PartitionSpec as P
from jax.experimental import pallas as pl
from jax.experimental.pallas import tpu as pltpu

sound_speed = 1.0
radial_rate = 0.2
azimuth_rate = 0.2
exact = lax.Precision.HIGHEST


def passed_along(block, axis, distance):
    devices = range(lax.axis_size(axis))
    route = [((i - distance) % len(devices), i) for i in devices]
    return lax.ppermute(block, axis, route)


def with_halo(cells, sides, width, closed):
    for axis, dim in sides:
        count = lax.axis_size(axis)
        ends = count if closed else count - 1
        head = lax.slice_in_dim(cells, 0, width, axis=dim)
        tail = lax.slice_in_dim(cells, cells.shape[dim] - width, cells.shape[dim], axis=dim)
        cells = jnp.concatenate(
            [
                lax.ppermute(tail, axis, [(i, (i + 1) % count) for i in range(ends)]),
                cells,
                lax.ppermute(head, axis, [((i + 1) % count, i) for i in range(ends)]),
            ],
            axis=dim,
        )
    return cells


def limited_slope(left_step, right_step):
    return (
        0.5
        * (jnp.sign(left_step) + jnp.sign(right_step))
        * jnp.minimum(jnp.abs(left_step), jnp.abs(right_step))
    )


def plm_divergence(values, speed, along_axis, extent):

    def take_range(source, offset_at, length):
        return lax.slice_in_dim(source, offset_at, offset_at + length, axis=along_axis)

    left_step = take_range(values, 1, extent + 2) - take_range(values, 0, extent + 2)
    right_step = take_range(values, 2, extent + 2) - take_range(values, 1, extent + 2)
    slopes = limited_slope(left_step, right_step)
    centre = take_range(values, 1, extent + 2)
    left_value = take_range(centre, 0, extent + 1) + 0.5 * take_range(slopes, 0, extent + 1)
    right_value = take_range(centre, 1, extent + 1) - 0.5 * take_range(slopes, 1, extent + 1)
    face_speed = 0.5 * (take_range(speed, 1, extent + 1) + take_range(speed, 2, extent + 1))
    face_flux = face_speed * 0.5 * (left_value + right_value) - 0.5 * (
        jnp.abs(face_speed) + sound_speed
    ) * (right_value - left_value)
    return take_range(face_flux, 1, extent) - take_range(face_flux, 0, extent)


def sector_roll(ring, quotient, remainder):
    sectors, per_member, rows, sector = ring.shape

    def kernel(quotient_ref, remainder_ref, ring_ref, out_ref):
        for i in range(per_member):
            whole = quotient_ref[i]
            part = remainder_ref[i]

            def body(s, carry):
                current = ring_ref[(s - whole + sectors) % sectors, i]
                preceding = ring_ref[(s - whole - 1 + 2 * sectors) % sectors, i]
                window = jnp.concatenate([preceding, current], axis=-1)
                out_ref[s, i] = pltpu.roll(window, part, 1)[:, sector:]
                return carry

            lax.fori_loop(0, sectors, body, 0)

    return pl.pallas_call(
        kernel,
        out_shape=jax.ShapeDtypeStruct(ring.shape, ring.dtype),
        in_specs=[
            pl.BlockSpec(memory_space=pltpu.SMEM),
            pl.BlockSpec(memory_space=pltpu.SMEM),
            pl.BlockSpec(memory_space=pltpu.VMEM),
        ],
        out_specs=pl.BlockSpec(memory_space=pltpu.VMEM),
    )(quotient, remainder, ring)


def local(
    gas_fields,
    orbit_shift,
    particle_velocity,
    particle_mass,
    particle_stop,
    particle_cell,
    particle_dest,
):
    field_count, radius_count, layers, sector = gas_fields.shape
    sectors = lax.axis_size("sec")
    per_member = radius_count // sectors
    member = lax.axis_index("sec")
    by_radius = gas_fields.transpose(1, 0, 2, 3)
    ring = lax.all_to_all(by_radius, "sec", split_axis=0, concat_axis=0, tiled=True)
    ring = ring.reshape(sectors, per_member, field_count * layers, sector)
    own_shift = lax.dynamic_slice_in_dim(orbit_shift, member * per_member, per_member)
    rolled = sector_roll(ring, own_shift // sector, own_shift % sector)
    rolled = rolled.reshape(sectors * per_member, field_count, layers, sector)
    shifted = lax.all_to_all(rolled, "sec", split_axis=0, concat_axis=0, tiled=True)
    shifted = shifted.transpose(1, 0, 2, 3)
    per_device = particle_dest.shape[0]
    devices = lax.axis_size(("rad", "sec"))
    capacity = 2 * per_device // devices
    target = particle_dest[:, 0]
    hits = target[:, None] == jnp.arange(devices, dtype=jnp.int32)[None, :]
    block_rows = min(128, per_device)
    block_count = per_device // block_rows
    hit_blocks = hits.astype(jnp.bfloat16).reshape(block_count, block_rows, devices)
    row_index = jnp.arange(block_rows, dtype=jnp.int32)
    within = (row_index[:, None] >= row_index[None, :]).astype(jnp.bfloat16)
    block_index = jnp.arange(block_count, dtype=jnp.int32)
    before = (block_index[:, None] > block_index[None, :]).astype(jnp.bfloat16)
    block_totals = jnp.sum(hit_blocks, axis=1, dtype=jnp.float32).astype(jnp.bfloat16)
    running = jnp.einsum(
        "ij,bjd->bid", within, hit_blocks, preferred_element_type=jnp.float32
    ) + jnp.dot(before, block_totals, preferred_element_type=jnp.float32)[:, None, :]
    running = running.reshape(per_device, devices)
    slot = jnp.sum(jnp.where(hits, running, 0.0), axis=1).astype(jnp.int32) - 1
    records = jnp.concatenate(
        [
            particle_velocity,
            particle_mass[None],
            particle_stop[None],
            particle_cell[None].astype(jnp.float32),
        ],
        axis=0,
    )
    slot_hot = slot[:, None] == jnp.arange(capacity, dtype=jnp.int32)[None, :]
    spread_records = jnp.where(slot_hot[:, None, :], records.T[:, :, None], 0.0).reshape(
        per_device, 6 * capacity
    )
    outbox = jnp.dot(
        hits.astype(jnp.float32).T, spread_records, precision=exact, preferred_element_type=jnp.float32
    ).reshape(devices, 6, capacity)
    inbox = lax.all_to_all(outbox, ("rad", "sec"), split_axis=0, concat_axis=0, tiled=True)
    received = inbox.transpose(1, 0, 2).reshape(6, devices * capacity)
    row_count = radius_count * layers
    velocity_rows = (
        (shifted[1:4] / shifted[0:1])
        .reshape(3, row_count, sector)
        .transpose(1, 0, 2)
        .reshape(row_count, 3 * sector)
    )
    cells = received[5].astype(jnp.int32)
    row_hot = (
        (cells // sector)[:, None] == jnp.arange(row_count, dtype=jnp.int32)[None, :]
    ).astype(jnp.float32)
    azimuth_hot = (
        (cells % sector)[:, None] == jnp.arange(sector, dtype=jnp.int32)[None, :]
    ).astype(jnp.float32)
    picked = jnp.dot(
        row_hot, velocity_rows, precision=lax.Precision.HIGH, preferred_element_type=jnp.float32
    ).reshape(-1, 3, sector)
    local_speed = jnp.sum(picked * azimuth_hot[:, None, :], axis=2).T
    velocity_in = received[0:3]
    fraction = received[4] / (1.0 + received[4])
    change = (velocity_in - local_speed) * fraction[None]
    arrived_velocity = velocity_in - change
    impulse = received[3][None] * change
    spread = (impulse.T[:, :, None] * azimuth_hot[:, None, :]).reshape(-1, 3 * sector)
    deposit_rows = jnp.dot(row_hot.T, spread, precision=lax.Precision.HIGH, preferred_element_type=jnp.float32)
    momentum_added = (
        deposit_rows.reshape(row_count, 3, sector)
        .transpose(1, 0, 2)
        .reshape(3, radius_count, layers, sector)
    )
    dragged = jnp.concatenate([shifted[0:1], shifted[1:4] + momentum_added, shifted[4:5]], axis=0)
    radial_speed = dragged[1] / dragged[0]
    azimuthal_speed = dragged[2] / dragged[0]
    stacked = jnp.concatenate([dragged, radial_speed[None], azimuthal_speed[None]], axis=0)
    radial_pad = with_halo(stacked, (("rad", 1),), 2, False)
    azimuth_pad = with_halo(stacked, (("sec", 3),), 2, True)
    radial_change = plm_divergence(radial_pad[0:5], radial_pad[5:6], 1, radius_count)
    azimuth_change = plm_divergence(azimuth_pad[0:5], azimuth_pad[6:7], 3, sector)
    gas_next = dragged - radial_rate * radial_change - azimuth_rate * azimuth_change
    return (gas_next, arrived_velocity)


def solution(mesh):
    placed = (
        P(None, "rad", None, "sec"),
        P("rad"),
        P(None, ("rad", "sec")),
        P(("rad", "sec")),
        P(("rad", "sec")),
        P(("rad", "sec")),
        P(("rad", "sec"), None),
    )
    return jax.shard_map(
        local,
        mesh=mesh,
        in_specs=placed,
        out_specs=(P(None, "rad", None, "sec"), P(None, ("rad", "sec"))),
        check_vma=False,
    )
```

```python
import jax
import jax.numpy as jnp
from jax import lax
from jax.sharding import PartitionSpec as P
from jax.experimental import pallas as pl
from jax.experimental.pallas import tpu as pltpu

sound_speed = 1.0
radial_rate = 0.2
azimuth_rate = 0.2
exact = lax.Precision.HIGHEST


def passed_along(block, axis, distance):
    devices = range(lax.axis_size(axis))
    route = [((i - distance) % len(devices), i) for i in devices]
    return lax.ppermute(block, axis, route)


def with_halo(cells, sides, width, closed):
    for axis, dim in sides:
        count = lax.axis_size(axis)
        ends = count if closed else count - 1
        head = lax.slice_in_dim(cells, 0, width, axis=dim)
        tail = lax.slice_in_dim(cells, cells.shape[dim] - width, cells.shape[dim], axis=dim)
        cells = jnp.concatenate(
            [
                lax.ppermute(tail, axis, [(i, (i + 1) % count) for i in range(ends)]),
                cells,
                lax.ppermute(head, axis, [((i + 1) % count, i) for i in range(ends)]),
            ],
            axis=dim,
        )
    return cells


def limited_slope(left_step, right_step):
    return (
        0.5
        * (jnp.sign(left_step) + jnp.sign(right_step))
        * jnp.minimum(jnp.abs(left_step), jnp.abs(right_step))
    )


def plm_divergence(values, speed, along_axis, extent):

    def take_range(source, offset_at, length):
        return lax.slice_in_dim(source, offset_at, offset_at + length, axis=along_axis)

    left_step = take_range(values, 1, extent + 2) - take_range(values, 0, extent + 2)
    right_step = take_range(values, 2, extent + 2) - take_range(values, 1, extent + 2)
    slopes = limited_slope(left_step, right_step)
    centre = take_range(values, 1, extent + 2)
    left_value = take_range(centre, 0, extent + 1) + 0.5 * take_range(slopes, 0, extent + 1)
    right_value = take_range(centre, 1, extent + 1) - 0.5 * take_range(slopes, 1, extent + 1)
    face_speed = 0.5 * (take_range(speed, 1, extent + 1) + take_range(speed, 2, extent + 1))
    face_flux = face_speed * 0.5 * (left_value + right_value) - 0.5 * (
        jnp.abs(face_speed) + sound_speed
    ) * (right_value - left_value)
    return take_range(face_flux, 1, extent) - take_range(face_flux, 0, extent)


def sector_roll(ring, quotient, remainder, passengers):
    sectors, per_member, rows, sector = ring.shape
    gas_rows = per_member * rows

    def kernel(quotient_ref, remainder_ref, ring_ref, passenger_ref, out_ref):
        out_ref[:, gas_rows:, :] = passenger_ref[...]
        for i in range(per_member):
            whole = quotient_ref[i]
            part = remainder_ref[i]

            def body(s, carry):
                current = ring_ref[(s - whole + sectors) % sectors, i]
                preceding = ring_ref[(s - whole - 1 + 2 * sectors) % sectors, i]
                window = jnp.concatenate([preceding, current], axis=-1)
                out_ref[s, i * rows : (i + 1) * rows] = pltpu.roll(window, part, 1)[:, sector:]
                return carry

            lax.fori_loop(0, sectors, body, 0)

    return pl.pallas_call(
        kernel,
        out_shape=jax.ShapeDtypeStruct(
            (sectors, gas_rows + passengers.shape[1], sector), ring.dtype
        ),
        in_specs=[
            pl.BlockSpec(memory_space=pltpu.SMEM),
            pl.BlockSpec(memory_space=pltpu.SMEM),
            pl.BlockSpec(memory_space=pltpu.VMEM),
            pl.BlockSpec(memory_space=pltpu.VMEM),
        ],
        out_specs=pl.BlockSpec(memory_space=pltpu.VMEM),
    )(quotient, remainder, ring, passengers)


def local(
    gas_fields,
    orbit_shift,
    particle_velocity,
    particle_mass,
    particle_stop,
    particle_cell,
    particle_dest,
):
    field_count, radius_count, layers, sector = gas_fields.shape
    sectors = lax.axis_size("sec")
    per_member = radius_count // sectors
    member = lax.axis_index("sec")
    per_device = particle_dest.shape[0]
    devices = lax.axis_size(("rad", "sec"))
    capacity = 2 * per_device // devices
    target = particle_dest[:, 0]
    hits = target[:, None] == jnp.arange(devices, dtype=jnp.int32)[None, :]
    block_rows = min(128, per_device)
    block_count = per_device // block_rows
    hit_blocks = hits.astype(jnp.bfloat16).reshape(block_count, block_rows, devices)
    row_index = jnp.arange(block_rows, dtype=jnp.int32)
    within = (row_index[:, None] >= row_index[None, :]).astype(jnp.bfloat16)
    block_index = jnp.arange(block_count, dtype=jnp.int32)
    before = (block_index[:, None] > block_index[None, :]).astype(jnp.bfloat16)
    block_totals = jnp.sum(hit_blocks, axis=1, dtype=jnp.float32).astype(jnp.bfloat16)
    running = jnp.einsum(
        "ij,bjd->bid", within, hit_blocks, preferred_element_type=jnp.float32
    ) + jnp.dot(before, block_totals, preferred_element_type=jnp.float32)[:, None, :]
    running = running.reshape(per_device, devices)
    slot = jnp.sum(jnp.where(hits, running, 0.0), axis=1).astype(jnp.int32) - 1
    records = jnp.concatenate(
        [
            particle_velocity,
            particle_mass[None],
            particle_stop[None],
            particle_cell[None].astype(jnp.float32),
        ],
        axis=0,
    )
    slot_hot = slot[:, None] == jnp.arange(capacity, dtype=jnp.int32)[None, :]
    spread_records = jnp.where(slot_hot[:, None, :], records.T[:, :, None], 0.0).reshape(
        per_device, 6 * capacity
    )
    outbox = jnp.dot(
        hits.astype(jnp.float32).T, spread_records, precision=exact, preferred_element_type=jnp.float32
    ).reshape(devices, 6, capacity)
    rads = lax.axis_size("rad")
    staged = lax.all_to_all(
        outbox.reshape(rads, sectors, 6, capacity), "rad", split_axis=0, concat_axis=0, tiled=True
    )
    passengers = staged.transpose(1, 2, 0, 3).reshape(sectors, -1, sector)
    by_radius = gas_fields.transpose(1, 0, 2, 3)
    ring = lax.all_to_all(by_radius, "sec", split_axis=0, concat_axis=0, tiled=True)
    ring = ring.reshape(sectors, per_member, field_count * layers, sector)
    own_shift = lax.dynamic_slice_in_dim(orbit_shift, member * per_member, per_member)
    rolled = sector_roll(ring, own_shift // sector, own_shift % sector, passengers)
    arrived = lax.all_to_all(rolled, "sec", split_axis=0, concat_axis=0, tiled=True)
    gas_rows = per_member * field_count * layers
    shifted = (
        arrived[:, :gas_rows]
        .reshape(radius_count, field_count, layers, sector)
        .transpose(1, 0, 2, 3)
    )
    received = (
        arrived[:, gas_rows:]
        .reshape(sectors, 6, rads, capacity)
        .transpose(1, 2, 0, 3)
        .reshape(6, devices * capacity)
    )
    row_count = radius_count * layers
    velocity_rows = (
        (shifted[1:4] / shifted[0:1])
        .reshape(3, row_count, sector)
        .transpose(1, 0, 2)
        .reshape(row_count, 3 * sector)
    )
    cells = received[5].astype(jnp.int32)
    row_hot = (
        (cells // sector)[:, None] == jnp.arange(row_count, dtype=jnp.int32)[None, :]
    ).astype(jnp.float32)
    azimuth_hot = (
        (cells % sector)[:, None] == jnp.arange(sector, dtype=jnp.int32)[None, :]
    ).astype(jnp.float32)
    picked = jnp.dot(
        row_hot, velocity_rows, precision=lax.Precision.HIGH, preferred_element_type=jnp.float32
    ).reshape(-1, 3, sector)
    local_speed = jnp.sum(picked * azimuth_hot[:, None, :], axis=2).T
    velocity_in = received[0:3]
    fraction = received[4] / (1.0 + received[4])
    change = (velocity_in - local_speed) * fraction[None]
    arrived_velocity = velocity_in - change
    impulse = received[3][None] * change
    spread = (impulse.T[:, :, None] * azimuth_hot[:, None, :]).reshape(-1, 3 * sector)
    deposit_rows = jnp.dot(row_hot.T, spread, precision=lax.Precision.HIGH, preferred_element_type=jnp.float32)
    momentum_added = (
        deposit_rows.reshape(row_count, 3, sector)
        .transpose(1, 0, 2)
        .reshape(3, radius_count, layers, sector)
    )
    dragged = jnp.concatenate([shifted[0:1], shifted[1:4] + momentum_added, shifted[4:5]], axis=0)
    radial_speed = dragged[1] / dragged[0]
    azimuthal_speed = dragged[2] / dragged[0]
    stacked = jnp.concatenate([dragged, radial_speed[None], azimuthal_speed[None]], axis=0)
    radial_pad = with_halo(stacked, (("rad", 1),), 2, False)
    azimuth_pad = with_halo(stacked, (("sec", 3),), 2, True)
    radial_change = plm_divergence(radial_pad[0:5], radial_pad[5:6], 1, radius_count)
    azimuth_change = plm_divergence(azimuth_pad[0:5], azimuth_pad[6:7], 3, sector)
    gas_next = dragged - radial_rate * radial_change - azimuth_rate * azimuth_change
    return (gas_next, arrived_velocity)


def solution(mesh):
    placed = (
        P(None, "rad", None, "sec"),
        P("rad"),
        P(None, ("rad", "sec")),
        P(("rad", "sec")),
        P(("rad", "sec")),
        P(("rad", "sec")),
        P(("rad", "sec"), None),
    )
    return jax.shard_map(
        local,
        mesh=mesh,
        in_specs=placed,
        out_specs=(P(None, "rad", None, "sec"), P(None, ("rad", "sec"))),
        check_vma=False,
    )
```

```python
import jax
import jax.numpy as jnp
from jax import lax
from jax.sharding import PartitionSpec as P
from jax.experimental import pallas as pl
from jax.experimental.pallas import tpu as pltpu

sound_speed = 1.0
radial_rate = 0.2
azimuth_rate = 0.2
exact = lax.Precision.HIGHEST


def passed_along(block, axis, distance):
    devices = range(lax.axis_size(axis))
    route = [((i - distance) % len(devices), i) for i in devices]
    return lax.ppermute(block, axis, route)


def with_halo(cells, sides, width, closed):
    for axis, dim in sides:
        count = lax.axis_size(axis)
        ends = count if closed else count - 1
        head = lax.slice_in_dim(cells, 0, width, axis=dim)
        tail = lax.slice_in_dim(cells, cells.shape[dim] - width, cells.shape[dim], axis=dim)
        cells = jnp.concatenate(
            [
                lax.ppermute(tail, axis, [(i, (i + 1) % count) for i in range(ends)]),
                cells,
                lax.ppermute(head, axis, [((i + 1) % count, i) for i in range(ends)]),
            ],
            axis=dim,
        )
    return cells


def limited_slope(left_step, right_step):
    return (
        0.5
        * (jnp.sign(left_step) + jnp.sign(right_step))
        * jnp.minimum(jnp.abs(left_step), jnp.abs(right_step))
    )


def plm_divergence(values, speed, along_axis, extent):

    def take_range(source, offset_at, length):
        return lax.slice_in_dim(source, offset_at, offset_at + length, axis=along_axis)

    left_step = take_range(values, 1, extent + 2) - take_range(values, 0, extent + 2)
    right_step = take_range(values, 2, extent + 2) - take_range(values, 1, extent + 2)
    slopes = limited_slope(left_step, right_step)
    centre = take_range(values, 1, extent + 2)
    left_value = take_range(centre, 0, extent + 1) + 0.5 * take_range(slopes, 0, extent + 1)
    right_value = take_range(centre, 1, extent + 1) - 0.5 * take_range(slopes, 1, extent + 1)
    face_speed = 0.5 * (take_range(speed, 1, extent + 1) + take_range(speed, 2, extent + 1))
    face_flux = face_speed * 0.5 * (left_value + right_value) - 0.5 * (
        jnp.abs(face_speed) + sound_speed
    ) * (right_value - left_value)
    return take_range(face_flux, 1, extent) - take_range(face_flux, 0, extent)


def sector_roll(ring, quotient, remainder):
    sectors, per_member, rows, sector = ring.shape

    def kernel(quotient_ref, remainder_ref, ring_ref, out_ref):
        for i in range(per_member):
            whole = quotient_ref[i]
            part = remainder_ref[i]

            def body(s, carry):
                current = ring_ref[(s - whole + sectors) % sectors, i]
                preceding = ring_ref[(s - whole - 1 + 2 * sectors) % sectors, i]
                window = jnp.concatenate([preceding, current], axis=-1)
                out_ref[s, i] = pltpu.roll(window, part, 1)[:, sector:]
                return carry

            lax.fori_loop(0, sectors, body, 0)

    return pl.pallas_call(
        kernel,
        out_shape=jax.ShapeDtypeStruct(ring.shape, ring.dtype),
        in_specs=[
            pl.BlockSpec(memory_space=pltpu.SMEM),
            pl.BlockSpec(memory_space=pltpu.SMEM),
            pl.BlockSpec(memory_space=pltpu.VMEM),
        ],
        out_specs=pl.BlockSpec(memory_space=pltpu.VMEM),
    )(quotient, remainder, ring)


def sign_of(x):
    return jnp.where(x > 0, 1.0, jnp.where(x < 0, -1.0, 0.0))

def minmod(a, b):
    return 0.5 * (sign_of(a) + sign_of(b)) * jnp.minimum(jnp.abs(a), jnp.abs(b))

def face_divergence(v_m2, v_m1, v0, v_p1, v_p2, s_m1, s0, s_p1):
    slope_m1 = minmod(v_m1 - v_m2, v0 - v_m1)
    slope_0 = minmod(v0 - v_m1, v_p1 - v0)
    slope_p1 = minmod(v_p1 - v0, v_p2 - v_p1)
    def flux(left, right, w):
        return w * 0.5 * (left + right) - 0.5 * (jnp.abs(w) + 1.0) * (right - left)
    upper = flux(v0 + 0.5 * slope_0, v_p1 - 0.5 * slope_p1, 0.5 * (s0 + s_p1))
    lower = flux(v_m1 + 0.5 * slope_m1, v0 - 0.5 * slope_0, 0.5 * (s_m1 + s0))
    return upper - lower

def transport(dragged, speeds, radial_low, radial_high, ring_low, ring_high, rate_r, rate_a):
    fields, radii, layers, cells = dragged.shape

    def kernel(d_ref, s_ref, rl_ref, rh_ref, al_ref, ah_ref, out_ref):
        lane = lax.broadcasted_iota(jnp.int32, (layers, cells), 1)

        def radial_at(f, r, offset):
            k = r + offset
            inner = d_ref[f, jnp.clip(k, 0, radii - 1)] if f < fields else s_ref[0, jnp.clip(k, 0, radii - 1)]
            low = rl_ref[f, jnp.clip(k + 2, 0, 1)]
            high = rh_ref[f, jnp.clip(k - radii, 0, 1)]
            return jnp.where(k < 0, low, jnp.where(k >= radii, high, inner))

        def ring_at(centre, f, r, offset):
            if offset < 0:
                moved = pltpu.roll(centre, -offset, 1)
                for j in range(-offset):
                    edge = al_ref[f, r, :, 2 + offset + j : 3 + offset + j]
                    moved = jnp.where(lane == j, edge, moved)
            else:
                moved = pltpu.roll(centre, cells - offset, 1)
                for j in range(offset):
                    edge = ah_ref[f, r, :, j : j + 1]
                    moved = jnp.where(lane == cells - offset + j, edge, moved)
            return moved

        def body(r, carry):
            sr = s_ref[0, r]
            sa = s_ref[1, r]
            sr_m1 = radial_at(fields, r, -1)
            sr_p1 = radial_at(fields, r, 1)
            sa_m1 = ring_at(sa, fields + 1, r, -1)
            sa_p1 = ring_at(sa, fields + 1, r, 1)
            for f in range(fields):
                v0 = d_ref[f, r]
                radial = face_divergence(
                    radial_at(f, r, -2), radial_at(f, r, -1), v0, radial_at(f, r, 1), radial_at(f, r, 2),
                    sr_m1, sr, sr_p1,
                )
                azimuthal = face_divergence(
                    ring_at(v0, f, r, -2), ring_at(v0, f, r, -1), v0, ring_at(v0, f, r, 1), ring_at(v0, f, r, 2),
                    sa_m1, sa, sa_p1,
                )
                out_ref[f, r] = v0 - rate_r * radial - rate_a * azimuthal
            return carry

        lax.fori_loop(0, radii, body, 0)

    vmem = pl.BlockSpec(memory_space=pltpu.VMEM)
    return pl.pallas_call(
        kernel,
        out_shape=jax.ShapeDtypeStruct(dragged.shape, dragged.dtype),
        in_specs=[vmem] * 6,
        out_specs=vmem,
    )(dragged, speeds, radial_low, radial_high, ring_low, ring_high)


def local(
    gas_fields,
    orbit_shift,
    particle_velocity,
    particle_mass,
    particle_stop,
    particle_cell,
    particle_dest,
):
    field_count, radius_count, layers, sector = gas_fields.shape
    sectors = lax.axis_size("sec")
    per_member = radius_count // sectors
    member = lax.axis_index("sec")
    by_radius = gas_fields.transpose(1, 0, 2, 3)
    ring = lax.all_to_all(by_radius, "sec", split_axis=0, concat_axis=0, tiled=True)
    ring = ring.reshape(sectors, per_member, field_count * layers, sector)
    own_shift = lax.dynamic_slice_in_dim(orbit_shift, member * per_member, per_member)
    rolled = sector_roll(ring, own_shift // sector, own_shift % sector)
    rolled = rolled.reshape(sectors * per_member, field_count, layers, sector)
    shifted = lax.all_to_all(rolled, "sec", split_axis=0, concat_axis=0, tiled=True)
    shifted = shifted.transpose(1, 0, 2, 3)
    per_device = particle_dest.shape[0]
    devices = lax.axis_size(("rad", "sec"))
    capacity = 2 * per_device // devices
    target = particle_dest[:, 0]
    hits = target[:, None] == jnp.arange(devices, dtype=jnp.int32)[None, :]
    block_rows = min(128, per_device)
    block_count = per_device // block_rows
    hit_blocks = hits.astype(jnp.bfloat16).reshape(block_count, block_rows, devices)
    row_index = jnp.arange(block_rows, dtype=jnp.int32)
    within = (row_index[:, None] >= row_index[None, :]).astype(jnp.bfloat16)
    block_index = jnp.arange(block_count, dtype=jnp.int32)
    before = (block_index[:, None] > block_index[None, :]).astype(jnp.bfloat16)
    block_totals = jnp.sum(hit_blocks, axis=1, dtype=jnp.float32).astype(jnp.bfloat16)
    running = jnp.einsum(
        "ij,bjd->bid", within, hit_blocks, preferred_element_type=jnp.float32
    ) + jnp.dot(before, block_totals, preferred_element_type=jnp.float32)[:, None, :]
    running = running.reshape(per_device, devices)
    slot = jnp.sum(jnp.where(hits, running, 0.0), axis=1).astype(jnp.int32) - 1
    records = jnp.concatenate(
        [
            particle_velocity,
            particle_mass[None],
            particle_stop[None],
            particle_cell[None].astype(jnp.float32),
        ],
        axis=0,
    )
    slot_hot = slot[:, None] == jnp.arange(capacity, dtype=jnp.int32)[None, :]
    spread_records = jnp.where(slot_hot[:, None, :], records.T[:, :, None], 0.0).reshape(
        per_device, 6 * capacity
    )
    outbox = jnp.dot(
        hits.astype(jnp.float32).T, spread_records, precision=exact, preferred_element_type=jnp.float32
    ).reshape(devices, 6, capacity)
    inbox = lax.all_to_all(outbox, ("rad", "sec"), split_axis=0, concat_axis=0, tiled=True)
    received = inbox.transpose(1, 0, 2).reshape(6, devices * capacity)
    row_count = radius_count * layers
    velocity_rows = (
        (shifted[1:4] / shifted[0:1])
        .reshape(3, row_count, sector)
        .transpose(1, 0, 2)
        .reshape(row_count, 3 * sector)
    )
    cells = received[5].astype(jnp.int32)
    row_hot = (
        (cells // sector)[:, None] == jnp.arange(row_count, dtype=jnp.int32)[None, :]
    ).astype(jnp.float32)
    azimuth_hot = (
        (cells % sector)[:, None] == jnp.arange(sector, dtype=jnp.int32)[None, :]
    ).astype(jnp.float32)
    picked = jnp.dot(
        row_hot, velocity_rows, precision=lax.Precision.HIGH, preferred_element_type=jnp.float32
    ).reshape(-1, 3, sector)
    local_speed = jnp.sum(picked * azimuth_hot[:, None, :], axis=2).T
    velocity_in = received[0:3]
    fraction = received[4] / (1.0 + received[4])
    change = (velocity_in - local_speed) * fraction[None]
    arrived_velocity = velocity_in - change
    impulse = received[3][None] * change
    spread = (impulse.T[:, :, None] * azimuth_hot[:, None, :]).reshape(-1, 3 * sector)
    deposit_rows = jnp.dot(row_hot.T, spread, precision=lax.Precision.HIGH, preferred_element_type=jnp.float32)
    momentum_added = (
        deposit_rows.reshape(row_count, 3, sector)
        .transpose(1, 0, 2)
        .reshape(3, radius_count, layers, sector)
    )
    dragged = jnp.concatenate([shifted[0:1], shifted[1:4] + momentum_added, shifted[4:5]], axis=0)
    radial_speed = dragged[1] / dragged[0]
    azimuthal_speed = dragged[2] / dragged[0]
    speeds = jnp.stack([radial_speed, azimuthal_speed], axis=0)
    rads = lax.axis_size("rad")
    radial_low = lax.ppermute(
        jnp.concatenate([dragged[:, -2:], speeds[:, -2:]], axis=0),
        "rad",
        [(i, i + 1) for i in range(rads - 1)],
    )
    radial_high = lax.ppermute(
        jnp.concatenate([dragged[:, :2], speeds[:, :2]], axis=0),
        "rad",
        [(i + 1, i) for i in range(rads - 1)],
    )
    ring_low = lax.ppermute(
        jnp.concatenate([dragged[..., -2:], speeds[..., -2:]], axis=0),
        "sec",
        [(i, (i + 1) % sectors) for i in range(sectors)],
    )
    ring_high = lax.ppermute(
        jnp.concatenate([dragged[..., :2], speeds[..., :2]], axis=0),
        "sec",
        [((i + 1) % sectors, i) for i in range(sectors)],
    )
    gas_next = transport(
        dragged, speeds, radial_low, radial_high, ring_low, ring_high, radial_rate, azimuth_rate
    )
    return (gas_next, arrived_velocity)


def solution(mesh):
    placed = (
        P(None, "rad", None, "sec"),
        P("rad"),
        P(None, ("rad", "sec")),
        P(("rad", "sec")),
        P(("rad", "sec")),
        P(("rad", "sec")),
        P(("rad", "sec"), None),
    )
    return jax.shard_map(
        local,
        mesh=mesh,
        in_specs=placed,
        out_specs=(P(None, "rad", None, "sec"), P(None, ("rad", "sec"))),
        check_vma=False,
    )
```

```python
import jax
import jax.numpy as jnp
from jax import lax
from jax.sharding import PartitionSpec as P
from jax.experimental import pallas as pl
from jax.experimental.pallas import tpu as pltpu

sound_speed = 1.0
radial_rate = 0.2
azimuth_rate = 0.2
exact = lax.Precision.HIGHEST


def passed_along(block, axis, distance):
    devices = range(lax.axis_size(axis))
    route = [((i - distance) % len(devices), i) for i in devices]
    return lax.ppermute(block, axis, route)


def with_halo(cells, sides, width, closed):
    for axis, dim in sides:
        count = lax.axis_size(axis)
        ends = count if closed else count - 1
        head = lax.slice_in_dim(cells, 0, width, axis=dim)
        tail = lax.slice_in_dim(cells, cells.shape[dim] - width, cells.shape[dim], axis=dim)
        cells = jnp.concatenate(
            [
                lax.ppermute(tail, axis, [(i, (i + 1) % count) for i in range(ends)]),
                cells,
                lax.ppermute(head, axis, [((i + 1) % count, i) for i in range(ends)]),
            ],
            axis=dim,
        )
    return cells


def limited_slope(left_step, right_step):
    return (
        0.5
        * (jnp.sign(left_step) + jnp.sign(right_step))
        * jnp.minimum(jnp.abs(left_step), jnp.abs(right_step))
    )


def plm_divergence(values, speed, along_axis, extent):

    def take_range(source, offset_at, length):
        return lax.slice_in_dim(source, offset_at, offset_at + length, axis=along_axis)

    left_step = take_range(values, 1, extent + 2) - take_range(values, 0, extent + 2)
    right_step = take_range(values, 2, extent + 2) - take_range(values, 1, extent + 2)
    slopes = limited_slope(left_step, right_step)
    centre = take_range(values, 1, extent + 2)
    left_value = take_range(centre, 0, extent + 1) + 0.5 * take_range(slopes, 0, extent + 1)
    right_value = take_range(centre, 1, extent + 1) - 0.5 * take_range(slopes, 1, extent + 1)
    face_speed = 0.5 * (take_range(speed, 1, extent + 1) + take_range(speed, 2, extent + 1))
    face_flux = face_speed * 0.5 * (left_value + right_value) - 0.5 * (
        jnp.abs(face_speed) + sound_speed
    ) * (right_value - left_value)
    return take_range(face_flux, 1, extent) - take_range(face_flux, 0, extent)


def sector_roll(ring, quotient, remainder):
    sectors, per_member, rows, sector = ring.shape

    def kernel(quotient_ref, remainder_ref, ring_ref, out_ref):
        for i in range(per_member):
            whole = quotient_ref[i]
            part = remainder_ref[i]

            def body(s, carry):
                current = ring_ref[(s - whole + sectors) % sectors, i]
                preceding = ring_ref[(s - whole - 1 + 2 * sectors) % sectors, i]
                window = jnp.concatenate([preceding, current], axis=-1)
                out_ref[s, i] = pltpu.roll(window, part, 1)[:, sector:]
                return carry

            lax.fori_loop(0, sectors, body, 0)

    return pl.pallas_call(
        kernel,
        out_shape=jax.ShapeDtypeStruct(ring.shape, ring.dtype),
        in_specs=[
            pl.BlockSpec(memory_space=pltpu.SMEM),
            pl.BlockSpec(memory_space=pltpu.SMEM),
            pl.BlockSpec(memory_space=pltpu.VMEM),
        ],
        out_specs=pl.BlockSpec(memory_space=pltpu.VMEM),
    )(quotient, remainder, ring)


def sign_of(x):
    return jnp.where(x > 0, 1.0, jnp.where(x < 0, -1.0, 0.0))

def minmod(a, b):
    return 0.5 * (sign_of(a) + sign_of(b)) * jnp.minimum(jnp.abs(a), jnp.abs(b))

def face_divergence(v_m2, v_m1, v0, v_p1, v_p2, s_m1, s0, s_p1):
    slope_m1 = minmod(v_m1 - v_m2, v0 - v_m1)
    slope_0 = minmod(v0 - v_m1, v_p1 - v0)
    slope_p1 = minmod(v_p1 - v0, v_p2 - v_p1)
    def flux(left, right, w):
        return w * 0.5 * (left + right) - 0.5 * (jnp.abs(w) + 1.0) * (right - left)
    upper = flux(v0 + 0.5 * slope_0, v_p1 - 0.5 * slope_p1, 0.5 * (s0 + s_p1))
    lower = flux(v_m1 + 0.5 * slope_m1, v0 - 0.5 * slope_0, 0.5 * (s_m1 + s0))
    return upper - lower

def transport(dragged, speeds, radial_low, radial_high, ring_low, ring_high, rate_r, rate_a):
    fields, radii, layers, cells = dragged.shape

    def kernel(d_ref, s_ref, rl_ref, rh_ref, al_ref, ah_ref, out_ref):
        lane = lax.broadcasted_iota(jnp.int32, (layers, cells), 1)

        def radial_at(f, r, offset):
            k = r + offset
            inner = d_ref[f, jnp.clip(k, 0, radii - 1)]
            low = rl_ref[f, jnp.clip(k + 2, 0, 1)]
            high = rh_ref[f, jnp.clip(k - radii, 0, 1)]
            return jnp.where(k < 0, low, jnp.where(k >= radii, high, inner))

        def ring_at(centre, f, r, offset):
            if offset < 0:
                moved = pltpu.roll(centre, -offset, 1)
                for j in range(-offset):
                    edge = al_ref[f, r, :, 2 + offset + j : 3 + offset + j]
                    moved = jnp.where(lane == j, edge, moved)
            else:
                moved = pltpu.roll(centre, cells - offset, 1)
                for j in range(offset):
                    edge = ah_ref[f, r, :, j : j + 1]
                    moved = jnp.where(lane == cells - offset + j, edge, moved)
            return moved

        def speed_at(r, offset):
            k = r + offset
            inner = s_ref[0, jnp.clip(k, 0, radii - 1)]
            low = rl_ref[fields, jnp.clip(k + 2, 0, 1)]
            high = rh_ref[fields, jnp.clip(k - radii, 0, 1)]
            return jnp.where(k < 0, low, jnp.where(k >= radii, high, inner))

        def flux(left, right, w):
            return w * 0.5 * (left + right) - 0.5 * (jnp.abs(w) + 1.0) * (right - left)

        def field_pass(f, unused):
            v_m2 = radial_at(f, 0, -2)
            v_m1 = radial_at(f, 0, -1)
            v_0 = d_ref[f, 0]
            v_p1 = radial_at(f, 0, 1)
            s_m1 = speed_at(0, -1)
            s_0 = s_ref[0, 0]
            slope_m1 = minmod(v_m1 - v_m2, v_0 - v_m1)
            slope_0 = minmod(v_0 - v_m1, v_p1 - v_0)
            start = (v_0, v_p1, slope_0, flux(v_m1 + 0.5 * slope_m1, v_0 - 0.5 * slope_0, 0.5 * (s_m1 + s_0)), s_0)

            def body(r, carry):
                v_r, v_r1, slope_r, lower, s_r = carry
                v_r2 = radial_at(f, r, 2)
                s_r1 = speed_at(r, 1)
                slope_r1 = minmod(v_r1 - v_r, v_r2 - v_r1)
                upper = flux(v_r + 0.5 * slope_r, v_r1 - 0.5 * slope_r1, 0.5 * (s_r + s_r1))
                sa = s_ref[1, r]
                azimuthal = face_divergence(
                    ring_at(v_r, f, r, -2), ring_at(v_r, f, r, -1), v_r, ring_at(v_r, f, r, 1), ring_at(v_r, f, r, 2),
                    ring_at(sa, fields + 1, r, -1), sa, ring_at(sa, fields + 1, r, 1),
                )
                out_ref[f, r] = v_r - rate_r * (upper - lower) - rate_a * azimuthal
                return (v_r1, v_r2, slope_r1, upper, s_r1)

            lax.fori_loop(0, radii, body, start)
            return unused

        lax.fori_loop(0, fields, field_pass, 0)

    vmem = pl.BlockSpec(memory_space=pltpu.VMEM)
    return pl.pallas_call(
        kernel,
        out_shape=jax.ShapeDtypeStruct(dragged.shape, dragged.dtype),
        in_specs=[vmem] * 6,
        out_specs=vmem,
    )(dragged, speeds, radial_low, radial_high, ring_low, ring_high)


def local(
    gas_fields,
    orbit_shift,
    particle_velocity,
    particle_mass,
    particle_stop,
    particle_cell,
    particle_dest,
):
    field_count, radius_count, layers, sector = gas_fields.shape
    sectors = lax.axis_size("sec")
    per_member = radius_count // sectors
    member = lax.axis_index("sec")
    by_radius = gas_fields.transpose(1, 0, 2, 3)
    ring = lax.all_to_all(by_radius, "sec", split_axis=0, concat_axis=0, tiled=True)
    ring = ring.reshape(sectors, per_member, field_count * layers, sector)
    own_shift = lax.dynamic_slice_in_dim(orbit_shift, member * per_member, per_member)
    rolled = sector_roll(ring, own_shift // sector, own_shift % sector)
    rolled = rolled.reshape(sectors * per_member, field_count, layers, sector)
    shifted = lax.all_to_all(rolled, "sec", split_axis=0, concat_axis=0, tiled=True)
    shifted = shifted.transpose(1, 0, 2, 3)
    per_device = particle_dest.shape[0]
    devices = lax.axis_size(("rad", "sec"))
    capacity = 2 * per_device // devices
    target = particle_dest[:, 0]
    hits = target[:, None] == jnp.arange(devices, dtype=jnp.int32)[None, :]
    block_rows = min(128, per_device)
    block_count = per_device // block_rows
    hit_blocks = hits.astype(jnp.bfloat16).reshape(block_count, block_rows, devices)
    row_index = jnp.arange(block_rows, dtype=jnp.int32)
    within = (row_index[:, None] >= row_index[None, :]).astype(jnp.bfloat16)
    block_index = jnp.arange(block_count, dtype=jnp.int32)
    before = (block_index[:, None] > block_index[None, :]).astype(jnp.bfloat16)
    block_totals = jnp.sum(hit_blocks, axis=1, dtype=jnp.float32).astype(jnp.bfloat16)
    running = jnp.einsum(
        "ij,bjd->bid", within, hit_blocks, preferred_element_type=jnp.float32
    ) + jnp.dot(before, block_totals, preferred_element_type=jnp.float32)[:, None, :]
    running = running.reshape(per_device, devices)
    slot = jnp.sum(jnp.where(hits, running, 0.0), axis=1).astype(jnp.int32) - 1
    records = jnp.concatenate(
        [
            particle_velocity,
            particle_mass[None],
            particle_stop[None],
            particle_cell[None].astype(jnp.float32),
        ],
        axis=0,
    )
    slot_hot = slot[:, None] == jnp.arange(capacity, dtype=jnp.int32)[None, :]
    spread_records = jnp.where(slot_hot[:, None, :], records.T[:, :, None], 0.0).reshape(
        per_device, 6 * capacity
    )
    outbox = jnp.dot(
        hits.astype(jnp.float32).T, spread_records, precision=exact, preferred_element_type=jnp.float32
    ).reshape(devices, 6, capacity)
    inbox = lax.all_to_all(outbox, ("rad", "sec"), split_axis=0, concat_axis=0, tiled=True)
    received = inbox.transpose(1, 0, 2).reshape(6, devices * capacity)
    row_count = radius_count * layers
    velocity_rows = (
        (shifted[1:4] / shifted[0:1])
        .reshape(3, row_count, sector)
        .transpose(1, 0, 2)
        .reshape(row_count, 3 * sector)
    )
    cells = received[5].astype(jnp.int32)
    row_hot = (
        (cells // sector)[:, None] == jnp.arange(row_count, dtype=jnp.int32)[None, :]
    ).astype(jnp.float32)
    azimuth_hot = (
        (cells % sector)[:, None] == jnp.arange(sector, dtype=jnp.int32)[None, :]
    ).astype(jnp.float32)
    picked = jnp.dot(
        row_hot, velocity_rows, precision=lax.Precision.HIGH, preferred_element_type=jnp.float32
    ).reshape(-1, 3, sector)
    local_speed = jnp.sum(picked * azimuth_hot[:, None, :], axis=2).T
    velocity_in = received[0:3]
    fraction = received[4] / (1.0 + received[4])
    change = (velocity_in - local_speed) * fraction[None]
    arrived_velocity = velocity_in - change
    impulse = received[3][None] * change
    spread = (impulse.T[:, :, None] * azimuth_hot[:, None, :]).reshape(-1, 3 * sector)
    deposit_rows = jnp.dot(row_hot.T, spread, precision=lax.Precision.HIGH, preferred_element_type=jnp.float32)
    momentum_added = (
        deposit_rows.reshape(row_count, 3, sector)
        .transpose(1, 0, 2)
        .reshape(3, radius_count, layers, sector)
    )
    dragged = jnp.concatenate([shifted[0:1], shifted[1:4] + momentum_added, shifted[4:5]], axis=0)
    radial_speed = dragged[1] / dragged[0]
    azimuthal_speed = dragged[2] / dragged[0]
    speeds = jnp.stack([radial_speed, azimuthal_speed], axis=0)
    rads = lax.axis_size("rad")
    radial_low = lax.ppermute(
        jnp.concatenate([dragged[:, -2:], speeds[:, -2:]], axis=0),
        "rad",
        [(i, i + 1) for i in range(rads - 1)],
    )
    radial_high = lax.ppermute(
        jnp.concatenate([dragged[:, :2], speeds[:, :2]], axis=0),
        "rad",
        [(i + 1, i) for i in range(rads - 1)],
    )
    ring_low = lax.ppermute(
        jnp.concatenate([dragged[..., -2:], speeds[..., -2:]], axis=0),
        "sec",
        [(i, (i + 1) % sectors) for i in range(sectors)],
    )
    ring_high = lax.ppermute(
        jnp.concatenate([dragged[..., :2], speeds[..., :2]], axis=0),
        "sec",
        [((i + 1) % sectors, i) for i in range(sectors)],
    )
    gas_next = transport(
        dragged, speeds, radial_low, radial_high, ring_low, ring_high, radial_rate, azimuth_rate
    )
    return (gas_next, arrived_velocity)


def solution(mesh):
    placed = (
        P(None, "rad", None, "sec"),
        P("rad"),
        P(None, ("rad", "sec")),
        P(("rad", "sec")),
        P(("rad", "sec")),
        P(("rad", "sec")),
        P(("rad", "sec"), None),
    )
    return jax.shard_map(
        local,
        mesh=mesh,
        in_specs=placed,
        out_specs=(P(None, "rad", None, "sec"), P(None, ("rad", "sec"))),
        check_vma=False,
    )
```

```python
import jax
import jax.numpy as jnp
from jax import lax
from jax.sharding import PartitionSpec as P
from jax.experimental import pallas as pl
from jax.experimental.pallas import tpu as pltpu

sound_speed = 1.0
radial_rate = 0.2
azimuth_rate = 0.2
exact = lax.Precision.HIGHEST


def passed_along(block, axis, distance):
    devices = range(lax.axis_size(axis))
    route = [((i - distance) % len(devices), i) for i in devices]
    return lax.ppermute(block, axis, route)


def with_halo(cells, sides, width, closed):
    for axis, dim in sides:
        count = lax.axis_size(axis)
        ends = count if closed else count - 1
        head = lax.slice_in_dim(cells, 0, width, axis=dim)
        tail = lax.slice_in_dim(cells, cells.shape[dim] - width, cells.shape[dim], axis=dim)
        cells = jnp.concatenate(
            [
                lax.ppermute(tail, axis, [(i, (i + 1) % count) for i in range(ends)]),
                cells,
                lax.ppermute(head, axis, [((i + 1) % count, i) for i in range(ends)]),
            ],
            axis=dim,
        )
    return cells


def limited_slope(left_step, right_step):
    return (
        0.5
        * (jnp.sign(left_step) + jnp.sign(right_step))
        * jnp.minimum(jnp.abs(left_step), jnp.abs(right_step))
    )


def plm_divergence(values, speed, along_axis, extent):

    def take_range(source, offset_at, length):
        return lax.slice_in_dim(source, offset_at, offset_at + length, axis=along_axis)

    left_step = take_range(values, 1, extent + 2) - take_range(values, 0, extent + 2)
    right_step = take_range(values, 2, extent + 2) - take_range(values, 1, extent + 2)
    slopes = limited_slope(left_step, right_step)
    centre = take_range(values, 1, extent + 2)
    left_value = take_range(centre, 0, extent + 1) + 0.5 * take_range(slopes, 0, extent + 1)
    right_value = take_range(centre, 1, extent + 1) - 0.5 * take_range(slopes, 1, extent + 1)
    face_speed = 0.5 * (take_range(speed, 1, extent + 1) + take_range(speed, 2, extent + 1))
    face_flux = face_speed * 0.5 * (left_value + right_value) - 0.5 * (
        jnp.abs(face_speed) + sound_speed
    ) * (right_value - left_value)
    return take_range(face_flux, 1, extent) - take_range(face_flux, 0, extent)


def sector_roll(ring, quotient, remainder):
    sectors, per_member, rows, sector = ring.shape

    def kernel(quotient_ref, remainder_ref, ring_ref, out_ref):
        for i in range(per_member):
            whole = quotient_ref[i]
            part = remainder_ref[i]

            def body(s, carry):
                current = ring_ref[(s - whole + sectors) % sectors, i]
                preceding = ring_ref[(s - whole - 1 + 2 * sectors) % sectors, i]
                window = jnp.concatenate([preceding, current], axis=-1)
                out_ref[s, i] = pltpu.roll(window, part, 1)[:, sector:]
                return carry

            lax.fori_loop(0, sectors, body, 0)

    return pl.pallas_call(
        kernel,
        out_shape=jax.ShapeDtypeStruct(ring.shape, ring.dtype),
        in_specs=[
            pl.BlockSpec(memory_space=pltpu.SMEM),
            pl.BlockSpec(memory_space=pltpu.SMEM),
            pl.BlockSpec(memory_space=pltpu.VMEM),
        ],
        out_specs=pl.BlockSpec(memory_space=pltpu.VMEM),
    )(quotient, remainder, ring)


def minmod(a, b):
    return jnp.maximum(jnp.minimum(a, b), 0.0) + jnp.minimum(jnp.maximum(a, b), 0.0)

def face_divergence(v_m2, v_m1, v0, v_p1, v_p2, s_m1, s0, s_p1):
    slope_m1 = minmod(v_m1 - v_m2, v0 - v_m1)
    slope_0 = minmod(v0 - v_m1, v_p1 - v0)
    slope_p1 = minmod(v_p1 - v0, v_p2 - v_p1)
    def flux(left, right, w):
        return w * 0.5 * (left + right) - 0.5 * (jnp.abs(w) + 1.0) * (right - left)
    upper = flux(v0 + 0.5 * slope_0, v_p1 - 0.5 * slope_p1, 0.5 * (s0 + s_p1))
    lower = flux(v_m1 + 0.5 * slope_m1, v0 - 0.5 * slope_0, 0.5 * (s_m1 + s0))
    return upper - lower

def transport(dragged, speeds, radial_low, radial_high, ring_low, ring_high, rate_r, rate_a):
    fields, radii, layers, cells = dragged.shape

    def kernel(d_ref, s_ref, rl_ref, rh_ref, al_ref, ah_ref, out_ref):
        lane = lax.broadcasted_iota(jnp.int32, (layers, cells), 1)

        def radial_at(f, r, offset):
            k = r + offset
            inner = d_ref[f, jnp.clip(k, 0, radii - 1)] if f < fields else s_ref[0, jnp.clip(k, 0, radii - 1)]
            low = rl_ref[f, jnp.clip(k + 2, 0, 1)]
            high = rh_ref[f, jnp.clip(k - radii, 0, 1)]
            return jnp.where(k < 0, low, jnp.where(k >= radii, high, inner))

        def ring_at(centre, f, r, offset):
            if offset < 0:
                moved = pltpu.roll(centre, -offset, 1)
                for j in range(-offset):
                    edge = al_ref[f, r, :, 2 + offset + j : 3 + offset + j]
                    moved = jnp.where(lane == j, edge, moved)
            else:
                moved = pltpu.roll(centre, cells - offset, 1)
                for j in range(offset):
                    edge = ah_ref[f, r, :, j : j + 1]
                    moved = jnp.where(lane == cells - offset + j, edge, moved)
            return moved

        def body(r, carry):
            sr = s_ref[0, r]
            sa = s_ref[1, r]
            sr_m1 = radial_at(fields, r, -1)
            sr_p1 = radial_at(fields, r, 1)
            sa_m1 = ring_at(sa, fields + 1, r, -1)
            sa_p1 = ring_at(sa, fields + 1, r, 1)
            for f in range(fields):
                v0 = d_ref[f, r]
                radial = face_divergence(
                    radial_at(f, r, -2), radial_at(f, r, -1), v0, radial_at(f, r, 1), radial_at(f, r, 2),
                    sr_m1, sr, sr_p1,
                )
                azimuthal = face_divergence(
                    ring_at(v0, f, r, -2), ring_at(v0, f, r, -1), v0, ring_at(v0, f, r, 1), ring_at(v0, f, r, 2),
                    sa_m1, sa, sa_p1,
                )
                out_ref[f, r] = v0 - rate_r * radial - rate_a * azimuthal
            return carry

        lax.fori_loop(0, radii, body, 0)

    vmem = pl.BlockSpec(memory_space=pltpu.VMEM)
    return pl.pallas_call(
        kernel,
        out_shape=jax.ShapeDtypeStruct(dragged.shape, dragged.dtype),
        in_specs=[vmem] * 6,
        out_specs=vmem,
    )(dragged, speeds, radial_low, radial_high, ring_low, ring_high)


def local(
    gas_fields,
    orbit_shift,
    particle_velocity,
    particle_mass,
    particle_stop,
    particle_cell,
    particle_dest,
):
    field_count, radius_count, layers, sector = gas_fields.shape
    sectors = lax.axis_size("sec")
    per_member = radius_count // sectors
    member = lax.axis_index("sec")
    by_radius = gas_fields.transpose(1, 0, 2, 3)
    ring = lax.all_to_all(by_radius, "sec", split_axis=0, concat_axis=0, tiled=True)
    ring = ring.reshape(sectors, per_member, field_count * layers, sector)
    own_shift = lax.dynamic_slice_in_dim(orbit_shift, member * per_member, per_member)
    rolled = sector_roll(ring, own_shift // sector, own_shift % sector)
    rolled = rolled.reshape(sectors * per_member, field_count, layers, sector)
    shifted = lax.all_to_all(rolled, "sec", split_axis=0, concat_axis=0, tiled=True)
    shifted = shifted.transpose(1, 0, 2, 3)
    per_device = particle_dest.shape[0]
    devices = lax.axis_size(("rad", "sec"))
    capacity = 2 * per_device // devices
    target = particle_dest[:, 0]
    hits = target[:, None] == jnp.arange(devices, dtype=jnp.int32)[None, :]
    block_rows = min(128, per_device)
    block_count = per_device // block_rows
    hit_blocks = hits.astype(jnp.bfloat16).reshape(block_count, block_rows, devices)
    row_index = jnp.arange(block_rows, dtype=jnp.int32)
    within = (row_index[:, None] >= row_index[None, :]).astype(jnp.bfloat16)
    block_index = jnp.arange(block_count, dtype=jnp.int32)
    before = (block_index[:, None] > block_index[None, :]).astype(jnp.bfloat16)
    block_totals = jnp.sum(hit_blocks, axis=1, dtype=jnp.float32).astype(jnp.bfloat16)
    running = jnp.einsum(
        "ij,bjd->bid", within, hit_blocks, preferred_element_type=jnp.float32
    ) + jnp.dot(before, block_totals, preferred_element_type=jnp.float32)[:, None, :]
    running = running.reshape(per_device, devices)
    slot = jnp.sum(jnp.where(hits, running, 0.0), axis=1).astype(jnp.int32) - 1
    records = jnp.concatenate(
        [
            particle_velocity,
            particle_mass[None],
            particle_stop[None],
            particle_cell[None].astype(jnp.float32),
        ],
        axis=0,
    )
    slot_hot = slot[:, None] == jnp.arange(capacity, dtype=jnp.int32)[None, :]
    spread_records = jnp.where(slot_hot[:, None, :], records.T[:, :, None], 0.0).reshape(
        per_device, 6 * capacity
    )
    outbox = jnp.dot(
        hits.astype(jnp.float32).T, spread_records, precision=exact, preferred_element_type=jnp.float32
    ).reshape(devices, 6, capacity)
    inbox = lax.all_to_all(outbox, ("rad", "sec"), split_axis=0, concat_axis=0, tiled=True)
    received = inbox.transpose(1, 0, 2).reshape(6, devices * capacity)
    row_count = radius_count * layers
    velocity_rows = (
        (shifted[1:4] / shifted[0:1])
        .reshape(3, row_count, sector)
        .transpose(1, 0, 2)
        .reshape(row_count, 3 * sector)
    )
    cells = received[5].astype(jnp.int32)
    row_hot = (
        (cells // sector)[:, None] == jnp.arange(row_count, dtype=jnp.int32)[None, :]
    ).astype(jnp.float32)
    azimuth_hot = (
        (cells % sector)[:, None] == jnp.arange(sector, dtype=jnp.int32)[None, :]
    ).astype(jnp.float32)
    picked = jnp.dot(
        row_hot, velocity_rows, precision=lax.Precision.HIGH, preferred_element_type=jnp.float32
    ).reshape(-1, 3, sector)
    local_speed = jnp.sum(picked * azimuth_hot[:, None, :], axis=2).T
    velocity_in = received[0:3]
    fraction = received[4] / (1.0 + received[4])
    change = (velocity_in - local_speed) * fraction[None]
    arrived_velocity = velocity_in - change
    impulse = received[3][None] * change
    spread = (impulse.T[:, :, None] * azimuth_hot[:, None, :]).reshape(-1, 3 * sector)
    deposit_rows = jnp.dot(row_hot.T, spread, precision=lax.Precision.HIGH, preferred_element_type=jnp.float32)
    momentum_added = (
        deposit_rows.reshape(row_count, 3, sector)
        .transpose(1, 0, 2)
        .reshape(3, radius_count, layers, sector)
    )
    dragged = jnp.concatenate([shifted[0:1], shifted[1:4] + momentum_added, shifted[4:5]], axis=0)
    radial_speed = dragged[1] / dragged[0]
    azimuthal_speed = dragged[2] / dragged[0]
    speeds = jnp.stack([radial_speed, azimuthal_speed], axis=0)
    rads = lax.axis_size("rad")
    radial_low = lax.ppermute(
        jnp.concatenate([dragged[:, -2:], speeds[:, -2:]], axis=0),
        "rad",
        [(i, i + 1) for i in range(rads - 1)],
    )
    radial_high = lax.ppermute(
        jnp.concatenate([dragged[:, :2], speeds[:, :2]], axis=0),
        "rad",
        [(i + 1, i) for i in range(rads - 1)],
    )
    ring_low = lax.ppermute(
        jnp.concatenate([dragged[..., -2:], speeds[..., -2:]], axis=0),
        "sec",
        [(i, (i + 1) % sectors) for i in range(sectors)],
    )
    ring_high = lax.ppermute(
        jnp.concatenate([dragged[..., :2], speeds[..., :2]], axis=0),
        "sec",
        [((i + 1) % sectors, i) for i in range(sectors)],
    )
    gas_next = transport(
        dragged, speeds, radial_low, radial_high, ring_low, ring_high, radial_rate, azimuth_rate
    )
    return (gas_next, arrived_velocity)


def solution(mesh):
    placed = (
        P(None, "rad", None, "sec"),
        P("rad"),
        P(None, ("rad", "sec")),
        P(("rad", "sec")),
        P(("rad", "sec")),
        P(("rad", "sec")),
        P(("rad", "sec"), None),
    )
    return jax.shard_map(
        local,
        mesh=mesh,
        in_specs=placed,
        out_specs=(P(None, "rad", None, "sec"), P(None, ("rad", "sec"))),
        check_vma=False,
    )
```

```python
import jax
import jax.numpy as jnp
from jax import lax
from jax.sharding import PartitionSpec as P
from jax.experimental import pallas as pl
from jax.experimental.pallas import tpu as pltpu

sound_speed = 1.0
radial_rate = 0.2
azimuth_rate = 0.2
exact = lax.Precision.HIGHEST


def passed_along(block, axis, distance):
    devices = range(lax.axis_size(axis))
    route = [((i - distance) % len(devices), i) for i in devices]
    return lax.ppermute(block, axis, route)


def with_halo(cells, sides, width, closed):
    for axis, dim in sides:
        count = lax.axis_size(axis)
        ends = count if closed else count - 1
        head = lax.slice_in_dim(cells, 0, width, axis=dim)
        tail = lax.slice_in_dim(cells, cells.shape[dim] - width, cells.shape[dim], axis=dim)
        cells = jnp.concatenate(
            [
                lax.ppermute(tail, axis, [(i, (i + 1) % count) for i in range(ends)]),
                cells,
                lax.ppermute(head, axis, [((i + 1) % count, i) for i in range(ends)]),
            ],
            axis=dim,
        )
    return cells


def limited_slope(left_step, right_step):
    return (
        0.5
        * (jnp.sign(left_step) + jnp.sign(right_step))
        * jnp.minimum(jnp.abs(left_step), jnp.abs(right_step))
    )


def plm_divergence(values, speed, along_axis, extent):

    def take_range(source, offset_at, length):
        return lax.slice_in_dim(source, offset_at, offset_at + length, axis=along_axis)

    left_step = take_range(values, 1, extent + 2) - take_range(values, 0, extent + 2)
    right_step = take_range(values, 2, extent + 2) - take_range(values, 1, extent + 2)
    slopes = limited_slope(left_step, right_step)
    centre = take_range(values, 1, extent + 2)
    left_value = take_range(centre, 0, extent + 1) + 0.5 * take_range(slopes, 0, extent + 1)
    right_value = take_range(centre, 1, extent + 1) - 0.5 * take_range(slopes, 1, extent + 1)
    face_speed = 0.5 * (take_range(speed, 1, extent + 1) + take_range(speed, 2, extent + 1))
    face_flux = face_speed * 0.5 * (left_value + right_value) - 0.5 * (
        jnp.abs(face_speed) + sound_speed
    ) * (right_value - left_value)
    return take_range(face_flux, 1, extent) - take_range(face_flux, 0, extent)


def sector_roll(ring, quotient, remainder):
    sectors, per_member, rows, sector = ring.shape

    def kernel(quotient_ref, remainder_ref, ring_ref, out_ref):
        for i in range(per_member):
            whole = quotient_ref[i]
            part = remainder_ref[i]

            def body(s, carry):
                current = ring_ref[(s - whole + sectors) % sectors, i]
                preceding = ring_ref[(s - whole - 1 + 2 * sectors) % sectors, i]
                window = jnp.concatenate([preceding, current], axis=-1)
                out_ref[s, i] = pltpu.roll(window, part, 1)[:, sector:]
                return carry

            lax.fori_loop(0, sectors, body, 0)

    return pl.pallas_call(
        kernel,
        out_shape=jax.ShapeDtypeStruct(ring.shape, ring.dtype),
        in_specs=[
            pl.BlockSpec(memory_space=pltpu.SMEM),
            pl.BlockSpec(memory_space=pltpu.SMEM),
            pl.BlockSpec(memory_space=pltpu.VMEM),
        ],
        out_specs=pl.BlockSpec(memory_space=pltpu.VMEM),
    )(quotient, remainder, ring)


def minmod(a, b):
    return jnp.maximum(jnp.minimum(a, b), 0.0) + jnp.minimum(jnp.maximum(a, b), 0.0)

def face_divergence(v_m2, v_m1, v0, v_p1, v_p2, s_m1, s0, s_p1):
    slope_m1 = minmod(v_m1 - v_m2, v0 - v_m1)
    slope_0 = minmod(v0 - v_m1, v_p1 - v0)
    slope_p1 = minmod(v_p1 - v0, v_p2 - v_p1)
    def flux(left, right, w):
        return w * 0.5 * (left + right) - 0.5 * (jnp.abs(w) + 1.0) * (right - left)
    upper = flux(v0 + 0.5 * slope_0, v_p1 - 0.5 * slope_p1, 0.5 * (s0 + s_p1))
    lower = flux(v_m1 + 0.5 * slope_m1, v0 - 0.5 * slope_0, 0.5 * (s_m1 + s0))
    return upper - lower

def transport(dragged, speeds, radial_low, radial_high, ring_low, ring_high, rate_r, rate_a):
    radii, fields, layers, cells = dragged.shape

    def kernel(d_ref, s_ref, rl_ref, rh_ref, al_ref, ah_ref, out_ref):
        lane = lax.broadcasted_iota(jnp.int32, (layers, cells), 1)

        def radial_at(f, r, offset):
            k = r + offset
            inner = d_ref[jnp.clip(k, 0, radii - 1), f] if f < fields else s_ref[0, jnp.clip(k, 0, radii - 1)]
            low = rl_ref[f, jnp.clip(k + 2, 0, 1)]
            high = rh_ref[f, jnp.clip(k - radii, 0, 1)]
            return jnp.where(k < 0, low, jnp.where(k >= radii, high, inner))

        def ring_at(centre, f, r, offset):
            if offset < 0:
                moved = pltpu.roll(centre, -offset, 1)
                for j in range(-offset):
                    edge = al_ref[f, r, :, 2 + offset + j : 3 + offset + j]
                    moved = jnp.where(lane == j, edge, moved)
            else:
                moved = pltpu.roll(centre, cells - offset, 1)
                for j in range(offset):
                    edge = ah_ref[f, r, :, j : j + 1]
                    moved = jnp.where(lane == cells - offset + j, edge, moved)
            return moved

        def body(r, carry):
            sr = s_ref[0, r]
            sa = s_ref[1, r]
            sr_m1 = radial_at(fields, r, -1)
            sr_p1 = radial_at(fields, r, 1)
            sa_m1 = ring_at(sa, fields + 1, r, -1)
            sa_p1 = ring_at(sa, fields + 1, r, 1)
            for f in range(fields):
                v0 = d_ref[r, f]
                radial = face_divergence(
                    radial_at(f, r, -2), radial_at(f, r, -1), v0, radial_at(f, r, 1), radial_at(f, r, 2),
                    sr_m1, sr, sr_p1,
                )
                azimuthal = face_divergence(
                    ring_at(v0, f, r, -2), ring_at(v0, f, r, -1), v0, ring_at(v0, f, r, 1), ring_at(v0, f, r, 2),
                    sa_m1, sa, sa_p1,
                )
                out_ref[f, r] = v0 - rate_r * radial - rate_a * azimuthal
            return carry

        lax.fori_loop(0, radii, body, 0)

    vmem = pl.BlockSpec(memory_space=pltpu.VMEM)
    return pl.pallas_call(
        kernel,
        out_shape=jax.ShapeDtypeStruct((fields, radii, layers, cells), dragged.dtype),
        in_specs=[vmem] * 6,
        out_specs=vmem,
    )(dragged, speeds, radial_low, radial_high, ring_low, ring_high)


def local(
    gas_fields,
    orbit_shift,
    particle_velocity,
    particle_mass,
    particle_stop,
    particle_cell,
    particle_dest,
):
    field_count, radius_count, layers, sector = gas_fields.shape
    sectors = lax.axis_size("sec")
    per_member = radius_count // sectors
    member = lax.axis_index("sec")
    by_radius = gas_fields.transpose(1, 0, 2, 3)
    ring = lax.all_to_all(by_radius, "sec", split_axis=0, concat_axis=0, tiled=True)
    ring = ring.reshape(sectors, per_member, field_count * layers, sector)
    own_shift = lax.dynamic_slice_in_dim(orbit_shift, member * per_member, per_member)
    rolled = sector_roll(ring, own_shift // sector, own_shift % sector)
    rolled = rolled.reshape(sectors * per_member, field_count, layers, sector)
    shifted = lax.all_to_all(rolled, "sec", split_axis=0, concat_axis=0, tiled=True)
    per_device = particle_dest.shape[0]
    devices = lax.axis_size(("rad", "sec"))
    capacity = 2 * per_device // devices
    target = particle_dest[:, 0]
    hits = target[:, None] == jnp.arange(devices, dtype=jnp.int32)[None, :]
    block_rows = min(128, per_device)
    block_count = per_device // block_rows
    hit_blocks = hits.astype(jnp.bfloat16).reshape(block_count, block_rows, devices)
    row_index = jnp.arange(block_rows, dtype=jnp.int32)
    within = (row_index[:, None] >= row_index[None, :]).astype(jnp.bfloat16)
    block_index = jnp.arange(block_count, dtype=jnp.int32)
    before = (block_index[:, None] > block_index[None, :]).astype(jnp.bfloat16)
    block_totals = jnp.sum(hit_blocks, axis=1, dtype=jnp.float32).astype(jnp.bfloat16)
    running = jnp.einsum(
        "ij,bjd->bid", within, hit_blocks, preferred_element_type=jnp.float32
    ) + jnp.dot(before, block_totals, preferred_element_type=jnp.float32)[:, None, :]
    running = running.reshape(per_device, devices)
    slot = jnp.sum(jnp.where(hits, running, 0.0), axis=1).astype(jnp.int32) - 1
    records = jnp.concatenate(
        [
            particle_velocity,
            particle_mass[None],
            particle_stop[None],
            particle_cell[None].astype(jnp.float32),
        ],
        axis=0,
    )
    slot_hot = slot[:, None] == jnp.arange(capacity, dtype=jnp.int32)[None, :]
    spread_records = jnp.where(slot_hot[:, None, :], records.T[:, :, None], 0.0).reshape(
        per_device, 6 * capacity
    )
    outbox = jnp.dot(
        hits.astype(jnp.float32).T, spread_records, precision=exact, preferred_element_type=jnp.float32
    ).reshape(devices, 6, capacity)
    inbox = lax.all_to_all(outbox, ("rad", "sec"), split_axis=0, concat_axis=0, tiled=True)
    received = inbox.transpose(1, 0, 2).reshape(6, devices * capacity)
    row_count = radius_count * layers
    cells = received[5].astype(jnp.int32)
    row_hot = (
        (cells // sector)[:, None] == jnp.arange(row_count, dtype=jnp.int32)[None, :]
    ).astype(jnp.float32)
    azimuth_hot = (
        (cells % sector)[:, None] == jnp.arange(sector, dtype=jnp.int32)[None, :]
    ).astype(jnp.float32)
    density = shifted[:, 0].reshape(row_count, sector)
    local_speed = jnp.stack(
        [
            jnp.sum(
                jnp.dot(
                    row_hot,
                    shifted[:, 1 + k].reshape(row_count, sector) / density,
                    precision=lax.Precision.HIGH,
                    preferred_element_type=jnp.float32,
                )
                * azimuth_hot,
                axis=1,
            )
            for k in range(3)
        ],
        axis=0,
    )
    velocity_in = received[0:3]
    fraction = received[4] / (1.0 + received[4])
    change = (velocity_in - local_speed) * fraction[None]
    arrived_velocity = velocity_in - change
    impulse = received[3][None] * change
    momentum_added = [
        jnp.dot(
            row_hot.T,
            impulse[k][:, None] * azimuth_hot,
            precision=lax.Precision.HIGH,
            preferred_element_type=jnp.float32,
        ).reshape(radius_count, layers, sector)
        for k in range(3)
    ]
    dragged = jnp.stack(
        [shifted[:, 0]] + [shifted[:, 1 + k] + momentum_added[k] for k in range(3)] + [shifted[:, 4]],
        axis=1,
    )
    radial_speed = dragged[:, 1] / dragged[:, 0]
    azimuthal_speed = dragged[:, 2] / dragged[:, 0]
    speeds = jnp.stack([radial_speed, azimuthal_speed], axis=0)
    rads = lax.axis_size("rad")
    radial_low = lax.ppermute(
        jnp.concatenate([dragged[-2:].transpose(1, 0, 2, 3), speeds[:, -2:]], axis=0),
        "rad",
        [(i, i + 1) for i in range(rads - 1)],
    )
    radial_high = lax.ppermute(
        jnp.concatenate([dragged[:2].transpose(1, 0, 2, 3), speeds[:, :2]], axis=0),
        "rad",
        [(i + 1, i) for i in range(rads - 1)],
    )
    ring_low = lax.ppermute(
        jnp.concatenate([dragged[..., -2:].transpose(1, 0, 2, 3), speeds[..., -2:]], axis=0),
        "sec",
        [(i, (i + 1) % sectors) for i in range(sectors)],
    )
    ring_high = lax.ppermute(
        jnp.concatenate([dragged[..., :2].transpose(1, 0, 2, 3), speeds[..., :2]], axis=0),
        "sec",
        [((i + 1) % sectors, i) for i in range(sectors)],
    )
    gas_next = transport(
        dragged, speeds, radial_low, radial_high, ring_low, ring_high, radial_rate, azimuth_rate
    )
    return (gas_next, arrived_velocity)


def solution(mesh):
    placed = (
        P(None, "rad", None, "sec"),
        P("rad"),
        P(None, ("rad", "sec")),
        P(("rad", "sec")),
        P(("rad", "sec")),
        P(("rad", "sec")),
        P(("rad", "sec"), None),
    )
    return jax.shard_map(
        local,
        mesh=mesh,
        in_specs=placed,
        out_specs=(P(None, "rad", None, "sec"), P(None, ("rad", "sec"))),
        check_vma=False,
    )
```

```python
import jax
import jax.numpy as jnp
from jax import lax
from jax.sharding import PartitionSpec as P
from jax.experimental import pallas as pl
from jax.experimental.pallas import tpu as pltpu

sound_speed = 1.0
radial_rate = 0.2
azimuth_rate = 0.2
exact = lax.Precision.HIGHEST


def passed_along(block, axis, distance):
    devices = range(lax.axis_size(axis))
    route = [((i - distance) % len(devices), i) for i in devices]
    return lax.ppermute(block, axis, route)


def with_halo(cells, sides, width, closed):
    for axis, dim in sides:
        count = lax.axis_size(axis)
        ends = count if closed else count - 1
        head = lax.slice_in_dim(cells, 0, width, axis=dim)
        tail = lax.slice_in_dim(cells, cells.shape[dim] - width, cells.shape[dim], axis=dim)
        cells = jnp.concatenate(
            [
                lax.ppermute(tail, axis, [(i, (i + 1) % count) for i in range(ends)]),
                cells,
                lax.ppermute(head, axis, [((i + 1) % count, i) for i in range(ends)]),
            ],
            axis=dim,
        )
    return cells


def limited_slope(left_step, right_step):
    return (
        0.5
        * (jnp.sign(left_step) + jnp.sign(right_step))
        * jnp.minimum(jnp.abs(left_step), jnp.abs(right_step))
    )


def plm_divergence(values, speed, along_axis, extent):

    def take_range(source, offset_at, length):
        return lax.slice_in_dim(source, offset_at, offset_at + length, axis=along_axis)

    left_step = take_range(values, 1, extent + 2) - take_range(values, 0, extent + 2)
    right_step = take_range(values, 2, extent + 2) - take_range(values, 1, extent + 2)
    slopes = limited_slope(left_step, right_step)
    centre = take_range(values, 1, extent + 2)
    left_value = take_range(centre, 0, extent + 1) + 0.5 * take_range(slopes, 0, extent + 1)
    right_value = take_range(centre, 1, extent + 1) - 0.5 * take_range(slopes, 1, extent + 1)
    face_speed = 0.5 * (take_range(speed, 1, extent + 1) + take_range(speed, 2, extent + 1))
    face_flux = face_speed * 0.5 * (left_value + right_value) - 0.5 * (
        jnp.abs(face_speed) + sound_speed
    ) * (right_value - left_value)
    return take_range(face_flux, 1, extent) - take_range(face_flux, 0, extent)


def sector_roll(ring, quotient, remainder):
    sectors, per_member, rows, sector = ring.shape

    def kernel(quotient_ref, remainder_ref, ring_ref, out_ref):
        for i in range(per_member):
            whole = quotient_ref[i]
            part = remainder_ref[i]

            tile = 128
            tiles = sector // tile
            offset = part // tile
            within = part % tile
            lane = lax.broadcasted_iota(jnp.int32, (rows, tile), 1)

            def body(s, carry):
                current = ring_ref[(s - whole + sectors) % sectors, i]
                preceding = ring_ref[(s - whole - 1 + 2 * sectors) % sectors, i]
                window = [preceding[:, t * tile : (t + 1) * tile] for t in range(tiles)] + [
                    current[:, t * tile : (t + 1) * tile] for t in range(tiles)
                ]

                def pick(index):
                    chosen = window[index]
                    for back in range(1, tiles):
                        if index - back >= 0:
                            chosen = jnp.where(offset == back, window[index - back], chosen)
                    return chosen

                pieces = []
                for t in range(tiles):
                    upper = pltpu.roll(pick(tiles + t), within, 1)
                    lower = pltpu.roll(pick(tiles + t - 1), within, 1)
                    pieces.append(jnp.where(lane >= within, upper, lower))
                out_ref[s, i] = jnp.concatenate(pieces, axis=-1)
                return carry

            lax.fori_loop(0, sectors, body, 0)

    return pl.pallas_call(
        kernel,
        out_shape=jax.ShapeDtypeStruct(ring.shape, ring.dtype),
        in_specs=[
            pl.BlockSpec(memory_space=pltpu.SMEM),
            pl.BlockSpec(memory_space=pltpu.SMEM),
            pl.BlockSpec(memory_space=pltpu.VMEM),
        ],
        out_specs=pl.BlockSpec(memory_space=pltpu.VMEM),
    )(quotient, remainder, ring)


def minmod(a, b):
    return jnp.maximum(jnp.minimum(a, b), 0.0) + jnp.minimum(jnp.maximum(a, b), 0.0)

def face_divergence(v_m2, v_m1, v0, v_p1, v_p2, s_m1, s0, s_p1):
    slope_m1 = minmod(v_m1 - v_m2, v0 - v_m1)
    slope_0 = minmod(v0 - v_m1, v_p1 - v0)
    slope_p1 = minmod(v_p1 - v0, v_p2 - v_p1)
    def flux(left, right, w):
        return w * 0.5 * (left + right) - 0.5 * (jnp.abs(w) + 1.0) * (right - left)
    upper = flux(v0 + 0.5 * slope_0, v_p1 - 0.5 * slope_p1, 0.5 * (s0 + s_p1))
    lower = flux(v_m1 + 0.5 * slope_m1, v0 - 0.5 * slope_0, 0.5 * (s_m1 + s0))
    return upper - lower

def transport(dragged, speeds, radial_low, radial_high, ring_low, ring_high, rate_r, rate_a):
    fields, radii, layers, cells = dragged.shape

    def kernel(d_ref, s_ref, rl_ref, rh_ref, al_ref, ah_ref, out_ref):
        lane = lax.broadcasted_iota(jnp.int32, (layers, cells), 1)

        def radial_at(f, r, offset):
            k = r + offset
            inner = d_ref[f, jnp.clip(k, 0, radii - 1)] if f < fields else s_ref[0, jnp.clip(k, 0, radii - 1)]
            low = rl_ref[f, jnp.clip(k + 2, 0, 1)]
            high = rh_ref[f, jnp.clip(k - radii, 0, 1)]
            return jnp.where(k < 0, low, jnp.where(k >= radii, high, inner))

        def ring_at(centre, f, r, offset):
            if offset < 0:
                moved = pltpu.roll(centre, -offset, 1)
                for j in range(-offset):
                    edge = al_ref[f, r, :, 2 + offset + j : 3 + offset + j]
                    moved = jnp.where(lane == j, edge, moved)
            else:
                moved = pltpu.roll(centre, cells - offset, 1)
                for j in range(offset):
                    edge = ah_ref[f, r, :, j : j + 1]
                    moved = jnp.where(lane == cells - offset + j, edge, moved)
            return moved

        def body(r, carry):
            sr = s_ref[0, r]
            sa = s_ref[1, r]
            sr_m1 = radial_at(fields, r, -1)
            sr_p1 = radial_at(fields, r, 1)
            sa_m1 = ring_at(sa, fields + 1, r, -1)
            sa_p1 = ring_at(sa, fields + 1, r, 1)
            for f in range(fields):
                v0 = d_ref[f, r]
                radial = face_divergence(
                    radial_at(f, r, -2), radial_at(f, r, -1), v0, radial_at(f, r, 1), radial_at(f, r, 2),
                    sr_m1, sr, sr_p1,
                )
                azimuthal = face_divergence(
                    ring_at(v0, f, r, -2), ring_at(v0, f, r, -1), v0, ring_at(v0, f, r, 1), ring_at(v0, f, r, 2),
                    sa_m1, sa, sa_p1,
                )
                out_ref[f, r] = v0 - rate_r * radial - rate_a * azimuthal
            return carry

        lax.fori_loop(0, radii, body, 0)

    vmem = pl.BlockSpec(memory_space=pltpu.VMEM)
    return pl.pallas_call(
        kernel,
        out_shape=jax.ShapeDtypeStruct(dragged.shape, dragged.dtype),
        in_specs=[vmem] * 6,
        out_specs=vmem,
    )(dragged, speeds, radial_low, radial_high, ring_low, ring_high)


def local(
    gas_fields,
    orbit_shift,
    particle_velocity,
    particle_mass,
    particle_stop,
    particle_cell,
    particle_dest,
):
    field_count, radius_count, layers, sector = gas_fields.shape
    sectors = lax.axis_size("sec")
    per_member = radius_count // sectors
    member = lax.axis_index("sec")
    by_radius = gas_fields.transpose(1, 0, 2, 3)
    ring = lax.all_to_all(by_radius, "sec", split_axis=0, concat_axis=0, tiled=True)
    ring = ring.reshape(sectors, per_member, field_count * layers, sector)
    own_shift = lax.dynamic_slice_in_dim(orbit_shift, member * per_member, per_member)
    rolled = sector_roll(ring, own_shift // sector, own_shift % sector)
    rolled = rolled.reshape(sectors * per_member, field_count, layers, sector)
    shifted = lax.all_to_all(rolled, "sec", split_axis=0, concat_axis=0, tiled=True)
    shifted = shifted.transpose(1, 0, 2, 3)
    per_device = particle_dest.shape[0]
    devices = lax.axis_size(("rad", "sec"))
    capacity = 2 * per_device // devices
    target = particle_dest[:, 0]
    hits = target[:, None] == jnp.arange(devices, dtype=jnp.int32)[None, :]
    block_rows = min(128, per_device)
    block_count = per_device // block_rows
    hit_blocks = hits.astype(jnp.bfloat16).reshape(block_count, block_rows, devices)
    row_index = jnp.arange(block_rows, dtype=jnp.int32)
    within = (row_index[:, None] >= row_index[None, :]).astype(jnp.bfloat16)
    block_index = jnp.arange(block_count, dtype=jnp.int32)
    before = (block_index[:, None] > block_index[None, :]).astype(jnp.bfloat16)
    block_totals = jnp.sum(hit_blocks, axis=1, dtype=jnp.float32).astype(jnp.bfloat16)
    running = jnp.einsum(
        "ij,bjd->bid", within, hit_blocks, preferred_element_type=jnp.float32
    ) + jnp.dot(before, block_totals, preferred_element_type=jnp.float32)[:, None, :]
    running = running.reshape(per_device, devices)
    slot = jnp.sum(jnp.where(hits, running, 0.0), axis=1).astype(jnp.int32) - 1
    records = jnp.concatenate(
        [
            particle_velocity,
            particle_mass[None],
            particle_stop[None],
            particle_cell[None].astype(jnp.float32),
        ],
        axis=0,
    )
    slot_hot = slot[:, None] == jnp.arange(capacity, dtype=jnp.int32)[None, :]
    spread_records = jnp.where(slot_hot[:, None, :], records.T[:, :, None], 0.0).reshape(
        per_device, 6 * capacity
    )
    outbox = jnp.dot(
        hits.astype(jnp.float32).T, spread_records, precision=exact, preferred_element_type=jnp.float32
    ).reshape(devices, 6, capacity)
    inbox = lax.all_to_all(outbox, ("rad", "sec"), split_axis=0, concat_axis=0, tiled=True)
    received = inbox.transpose(1, 0, 2).reshape(6, devices * capacity)
    row_count = radius_count * layers
    velocity_rows = (
        (shifted[1:4] / shifted[0:1])
        .reshape(3, row_count, sector)
        .transpose(1, 0, 2)
        .reshape(row_count, 3 * sector)
    )
    cells = received[5].astype(jnp.int32)
    row_hot = (
        (cells // sector)[:, None] == jnp.arange(row_count, dtype=jnp.int32)[None, :]
    ).astype(jnp.float32)
    azimuth_hot = (
        (cells % sector)[:, None] == jnp.arange(sector, dtype=jnp.int32)[None, :]
    ).astype(jnp.float32)
    picked = jnp.dot(
        row_hot, velocity_rows, precision=lax.Precision.HIGH, preferred_element_type=jnp.float32
    ).reshape(-1, 3, sector)
    local_speed = jnp.sum(picked * azimuth_hot[:, None, :], axis=2).T
    velocity_in = received[0:3]
    fraction = received[4] / (1.0 + received[4])
    change = (velocity_in - local_speed) * fraction[None]
    arrived_velocity = velocity_in - change
    impulse = received[3][None] * change
    spread = (impulse.T[:, :, None] * azimuth_hot[:, None, :]).reshape(-1, 3 * sector)
    deposit_rows = jnp.dot(row_hot.T, spread, precision=lax.Precision.HIGH, preferred_element_type=jnp.float32)
    momentum_added = (
        deposit_rows.reshape(row_count, 3, sector)
        .transpose(1, 0, 2)
        .reshape(3, radius_count, layers, sector)
    )
    dragged = jnp.concatenate([shifted[0:1], shifted[1:4] + momentum_added, shifted[4:5]], axis=0)
    radial_speed = dragged[1] / dragged[0]
    azimuthal_speed = dragged[2] / dragged[0]
    speeds = jnp.stack([radial_speed, azimuthal_speed], axis=0)
    rads = lax.axis_size("rad")
    radial_low = lax.ppermute(
        jnp.concatenate([dragged[:, -2:], speeds[:, -2:]], axis=0),
        "rad",
        [(i, i + 1) for i in range(rads - 1)],
    )
    radial_high = lax.ppermute(
        jnp.concatenate([dragged[:, :2], speeds[:, :2]], axis=0),
        "rad",
        [(i + 1, i) for i in range(rads - 1)],
    )
    ring_low = lax.ppermute(
        jnp.concatenate([dragged[..., -2:], speeds[..., -2:]], axis=0),
        "sec",
        [(i, (i + 1) % sectors) for i in range(sectors)],
    )
    ring_high = lax.ppermute(
        jnp.concatenate([dragged[..., :2], speeds[..., :2]], axis=0),
        "sec",
        [((i + 1) % sectors, i) for i in range(sectors)],
    )
    gas_next = transport(
        dragged, speeds, radial_low, radial_high, ring_low, ring_high, radial_rate, azimuth_rate
    )
    return (gas_next, arrived_velocity)


def solution(mesh):
    placed = (
        P(None, "rad", None, "sec"),
        P("rad"),
        P(None, ("rad", "sec")),
        P(("rad", "sec")),
        P(("rad", "sec")),
        P(("rad", "sec")),
        P(("rad", "sec"), None),
    )
    return jax.shard_map(
        local,
        mesh=mesh,
        in_specs=placed,
        out_specs=(P(None, "rad", None, "sec"), P(None, ("rad", "sec"))),
        check_vma=False,
    )
```

```python
import jax
import jax.numpy as jnp
from jax import lax
from jax.sharding import PartitionSpec as P
from jax.experimental import pallas as pl
from jax.experimental.pallas import tpu as pltpu

sound_speed = 1.0
radial_rate = 0.2
azimuth_rate = 0.2
exact = lax.Precision.HIGHEST


def passed_along(block, axis, distance):
    devices = range(lax.axis_size(axis))
    route = [((i - distance) % len(devices), i) for i in devices]
    return lax.ppermute(block, axis, route)


def with_halo(cells, sides, width, closed):
    for axis, dim in sides:
        count = lax.axis_size(axis)
        ends = count if closed else count - 1
        head = lax.slice_in_dim(cells, 0, width, axis=dim)
        tail = lax.slice_in_dim(cells, cells.shape[dim] - width, cells.shape[dim], axis=dim)
        cells = jnp.concatenate(
            [
                lax.ppermute(tail, axis, [(i, (i + 1) % count) for i in range(ends)]),
                cells,
                lax.ppermute(head, axis, [((i + 1) % count, i) for i in range(ends)]),
            ],
            axis=dim,
        )
    return cells


def limited_slope(left_step, right_step):
    return (
        0.5
        * (jnp.sign(left_step) + jnp.sign(right_step))
        * jnp.minimum(jnp.abs(left_step), jnp.abs(right_step))
    )


def plm_divergence(values, speed, along_axis, extent):

    def take_range(source, offset_at, length):
        return lax.slice_in_dim(source, offset_at, offset_at + length, axis=along_axis)

    left_step = take_range(values, 1, extent + 2) - take_range(values, 0, extent + 2)
    right_step = take_range(values, 2, extent + 2) - take_range(values, 1, extent + 2)
    slopes = limited_slope(left_step, right_step)
    centre = take_range(values, 1, extent + 2)
    left_value = take_range(centre, 0, extent + 1) + 0.5 * take_range(slopes, 0, extent + 1)
    right_value = take_range(centre, 1, extent + 1) - 0.5 * take_range(slopes, 1, extent + 1)
    face_speed = 0.5 * (take_range(speed, 1, extent + 1) + take_range(speed, 2, extent + 1))
    face_flux = face_speed * 0.5 * (left_value + right_value) - 0.5 * (
        jnp.abs(face_speed) + sound_speed
    ) * (right_value - left_value)
    return take_range(face_flux, 1, extent) - take_range(face_flux, 0, extent)


def sector_roll(ring, quotient, remainder):
    sectors, per_member, rows, sector = ring.shape

    def kernel(quotient_ref, remainder_ref, ring_ref, out_ref):
        for i in range(per_member):
            whole = quotient_ref[i]
            part = remainder_ref[i]

            tile = 128
            tiles = sector // tile
            offset = part // tile
            within = part % tile
            lane = lax.broadcasted_iota(jnp.int32, (rows, tile), 1)

            def body(s, carry):
                current = ring_ref[(s - whole + sectors) % sectors, i]
                preceding = ring_ref[(s - whole - 1 + 2 * sectors) % sectors, i]
                window = [preceding[:, t * tile : (t + 1) * tile] for t in range(tiles)] + [
                    current[:, t * tile : (t + 1) * tile] for t in range(tiles)
                ]

                def pick(index):
                    chosen = window[index]
                    for back in range(1, tiles):
                        if index - back >= 0:
                            chosen = jnp.where(offset == back, window[index - back], chosen)
                    return chosen

                pieces = []
                for t in range(tiles):
                    upper = pltpu.roll(pick(tiles + t), within, 1)
                    lower = pltpu.roll(pick(tiles + t - 1), within, 1)
                    pieces.append(jnp.where(lane >= within, upper, lower))
                out_ref[s, i] = jnp.concatenate(pieces, axis=-1)
                return carry

            lax.fori_loop(0, sectors, body, 0)

    return pl.pallas_call(
        kernel,
        out_shape=jax.ShapeDtypeStruct(ring.shape, ring.dtype),
        in_specs=[
            pl.BlockSpec(memory_space=pltpu.SMEM),
            pl.BlockSpec(memory_space=pltpu.SMEM),
            pl.BlockSpec(memory_space=pltpu.VMEM),
        ],
        out_specs=pl.BlockSpec(memory_space=pltpu.VMEM),
    )(quotient, remainder, ring)


def minmod(a, b):
    return jnp.maximum(jnp.minimum(a, b), 0.0) + jnp.minimum(jnp.maximum(a, b), 0.0)

def face_divergence(v_m2, v_m1, v0, v_p1, v_p2, s_m1, s0, s_p1):
    slope_m1 = minmod(v_m1 - v_m2, v0 - v_m1)
    slope_0 = minmod(v0 - v_m1, v_p1 - v0)
    slope_p1 = minmod(v_p1 - v0, v_p2 - v_p1)
    def flux(left, right, w):
        return w * 0.5 * (left + right) - 0.5 * (jnp.abs(w) + 1.0) * (right - left)
    upper = flux(v0 + 0.5 * slope_0, v_p1 - 0.5 * slope_p1, 0.5 * (s0 + s_p1))
    lower = flux(v_m1 + 0.5 * slope_m1, v0 - 0.5 * slope_0, 0.5 * (s_m1 + s0))
    return upper - lower

def transport(dragged, speeds, radial_low, radial_high, ring_low, ring_high, rate_r, rate_a):
    fields, radii, layers, cells = dragged.shape

    def kernel(d_ref, s_ref, rl_ref, rh_ref, al_ref, ah_ref, out_ref):
        lane = lax.broadcasted_iota(jnp.int32, (layers, cells), 1)

        def radial_at(f, r, offset):
            k = r + offset
            inner = d_ref[f, jnp.clip(k, 0, radii - 1)] if f < fields else s_ref[0, jnp.clip(k, 0, radii - 1)]
            low = rl_ref[f, jnp.clip(k + 2, 0, 1)]
            high = rh_ref[f, jnp.clip(k - radii, 0, 1)]
            return jnp.where(k < 0, low, jnp.where(k >= radii, high, inner))

        def ring_at(centre, f, r, offset):
            if offset < 0:
                moved = pltpu.roll(centre, -offset, 1)
                for j in range(-offset):
                    edge = al_ref[f, r, :, 2 + offset + j : 3 + offset + j]
                    moved = jnp.where(lane == j, edge, moved)
            else:
                moved = pltpu.roll(centre, cells - offset, 1)
                for j in range(offset):
                    edge = ah_ref[f, r, :, j : j + 1]
                    moved = jnp.where(lane == cells - offset + j, edge, moved)
            return moved

        def body(r, carry):
            sr = s_ref[0, r]
            sa = s_ref[1, r]
            sr_m1 = radial_at(fields, r, -1)
            sr_p1 = radial_at(fields, r, 1)
            sa_m1 = ring_at(sa, fields + 1, r, -1)
            sa_p1 = ring_at(sa, fields + 1, r, 1)
            for f in range(fields):
                v0 = d_ref[f, r]
                radial = face_divergence(
                    radial_at(f, r, -2), radial_at(f, r, -1), v0, radial_at(f, r, 1), radial_at(f, r, 2),
                    sr_m1, sr, sr_p1,
                )
                azimuthal = face_divergence(
                    ring_at(v0, f, r, -2), ring_at(v0, f, r, -1), v0, ring_at(v0, f, r, 1), ring_at(v0, f, r, 2),
                    sa_m1, sa, sa_p1,
                )
                out_ref[f, r] = v0 - rate_r * radial - rate_a * azimuthal
            return carry

        lax.fori_loop(0, radii, body, 0)

    vmem = pl.BlockSpec(memory_space=pltpu.VMEM)
    return pl.pallas_call(
        kernel,
        out_shape=jax.ShapeDtypeStruct(dragged.shape, dragged.dtype),
        in_specs=[vmem] * 6,
        out_specs=vmem,
    )(dragged, speeds, radial_low, radial_high, ring_low, ring_high)


def local(
    gas_fields,
    orbit_shift,
    particle_velocity,
    particle_mass,
    particle_stop,
    particle_cell,
    particle_dest,
):
    field_count, radius_count, layers, sector = gas_fields.shape
    sectors = lax.axis_size("sec")
    per_member = radius_count // sectors
    member = lax.axis_index("sec")
    by_radius = gas_fields.transpose(1, 0, 2, 3)
    ring = lax.all_to_all(by_radius, "sec", split_axis=0, concat_axis=0, tiled=True)
    ring = ring.reshape(sectors, per_member, field_count * layers, sector)
    own_shift = lax.dynamic_slice_in_dim(orbit_shift, member * per_member, per_member)
    rolled = sector_roll(ring, own_shift // sector, own_shift % sector)
    rolled = rolled.reshape(sectors * per_member, field_count, layers, sector)
    shifted = lax.all_to_all(rolled, "sec", split_axis=0, concat_axis=0, tiled=True)
    shifted = shifted.transpose(1, 0, 2, 3)
    per_device = particle_dest.shape[0]
    devices = lax.axis_size(("rad", "sec"))
    capacity = 2 * per_device // devices
    target = particle_dest[:, 0]
    hits = target[:, None] == jnp.arange(devices, dtype=jnp.int32)[None, :]
    block_rows = min(128, per_device)
    block_count = per_device // block_rows
    hit_blocks = hits.astype(jnp.bfloat16).reshape(block_count, block_rows, devices)
    row_index = jnp.arange(block_rows, dtype=jnp.int32)
    within = (row_index[:, None] >= row_index[None, :]).astype(jnp.bfloat16)
    block_index = jnp.arange(block_count, dtype=jnp.int32)
    before = (block_index[:, None] > block_index[None, :]).astype(jnp.bfloat16)
    block_totals = jnp.sum(hit_blocks, axis=1, dtype=jnp.float32).astype(jnp.bfloat16)
    running = jnp.einsum(
        "ij,bjd->bid", within, hit_blocks, preferred_element_type=jnp.float32
    ) + jnp.dot(before, block_totals, preferred_element_type=jnp.float32)[:, None, :]
    running = running.reshape(per_device, devices)
    slot = jnp.sum(jnp.where(hits, running, 0.0), axis=1).astype(jnp.int32) - 1
    records = jnp.concatenate(
        [
            particle_velocity,
            particle_mass[None],
            particle_stop[None],
            particle_cell[None].astype(jnp.float32),
        ],
        axis=0,
    )
    slot_hot = slot[:, None] == jnp.arange(capacity, dtype=jnp.int32)[None, :]
    spread_records = jnp.where(slot_hot[:, None, :], records.T[:, :, None], 0.0).reshape(
        per_device, 6 * capacity
    )
    outbox = jnp.dot(
        hits.astype(jnp.float32).T, spread_records, precision=exact, preferred_element_type=jnp.float32
    ).reshape(devices, 6, capacity)
    outbox, _ = lax.optimization_barrier((outbox, ring))
    inbox = lax.all_to_all(outbox, ("rad", "sec"), split_axis=0, concat_axis=0, tiled=True)
    received = inbox.transpose(1, 0, 2).reshape(6, devices * capacity)
    row_count = radius_count * layers
    velocity_rows = (
        (shifted[1:4] / shifted[0:1])
        .reshape(3, row_count, sector)
        .transpose(1, 0, 2)
        .reshape(row_count, 3 * sector)
    )
    cells = received[5].astype(jnp.int32)
    row_hot = (
        (cells // sector)[:, None] == jnp.arange(row_count, dtype=jnp.int32)[None, :]
    ).astype(jnp.float32)
    azimuth_hot = (
        (cells % sector)[:, None] == jnp.arange(sector, dtype=jnp.int32)[None, :]
    ).astype(jnp.float32)
    picked = jnp.dot(
        row_hot, velocity_rows, precision=lax.Precision.HIGH, preferred_element_type=jnp.float32
    ).reshape(-1, 3, sector)
    local_speed = jnp.sum(picked * azimuth_hot[:, None, :], axis=2).T
    velocity_in = received[0:3]
    fraction = received[4] / (1.0 + received[4])
    change = (velocity_in - local_speed) * fraction[None]
    arrived_velocity = velocity_in - change
    impulse = received[3][None] * change
    spread = (impulse.T[:, :, None] * azimuth_hot[:, None, :]).reshape(-1, 3 * sector)
    deposit_rows = jnp.dot(row_hot.T, spread, precision=lax.Precision.HIGH, preferred_element_type=jnp.float32)
    momentum_added = (
        deposit_rows.reshape(row_count, 3, sector)
        .transpose(1, 0, 2)
        .reshape(3, radius_count, layers, sector)
    )
    dragged = jnp.concatenate([shifted[0:1], shifted[1:4] + momentum_added, shifted[4:5]], axis=0)
    radial_speed = dragged[1] / dragged[0]
    azimuthal_speed = dragged[2] / dragged[0]
    speeds = jnp.stack([radial_speed, azimuthal_speed], axis=0)
    rads = lax.axis_size("rad")
    radial_low = lax.ppermute(
        jnp.concatenate([dragged[:, -2:], speeds[:, -2:]], axis=0),
        "rad",
        [(i, i + 1) for i in range(rads - 1)],
    )
    radial_high = lax.ppermute(
        jnp.concatenate([dragged[:, :2], speeds[:, :2]], axis=0),
        "rad",
        [(i + 1, i) for i in range(rads - 1)],
    )
    ring_low = lax.ppermute(
        jnp.concatenate([dragged[..., -2:], speeds[..., -2:]], axis=0),
        "sec",
        [(i, (i + 1) % sectors) for i in range(sectors)],
    )
    ring_high = lax.ppermute(
        jnp.concatenate([dragged[..., :2], speeds[..., :2]], axis=0),
        "sec",
        [((i + 1) % sectors, i) for i in range(sectors)],
    )
    gas_next = transport(
        dragged, speeds, radial_low, radial_high, ring_low, ring_high, radial_rate, azimuth_rate
    )
    return (gas_next, arrived_velocity)


def solution(mesh):
    placed = (
        P(None, "rad", None, "sec"),
        P("rad"),
        P(None, ("rad", "sec")),
        P(("rad", "sec")),
        P(("rad", "sec")),
        P(("rad", "sec")),
        P(("rad", "sec"), None),
    )
    return jax.shard_map(
        local,
        mesh=mesh,
        in_specs=placed,
        out_specs=(P(None, "rad", None, "sec"), P(None, ("rad", "sec"))),
        check_vma=False,
    )
```

```python
import jax
import jax.numpy as jnp
from jax import lax
from jax.sharding import PartitionSpec as P
from jax.experimental import pallas as pl
from jax.experimental.pallas import tpu as pltpu

sound_speed = 1.0
radial_rate = 0.2
azimuth_rate = 0.2
exact = lax.Precision.HIGHEST


def passed_along(block, axis, distance):
    devices = range(lax.axis_size(axis))
    route = [((i - distance) % len(devices), i) for i in devices]
    return lax.ppermute(block, axis, route)


def with_halo(cells, sides, width, closed):
    for axis, dim in sides:
        count = lax.axis_size(axis)
        ends = count if closed else count - 1
        head = lax.slice_in_dim(cells, 0, width, axis=dim)
        tail = lax.slice_in_dim(cells, cells.shape[dim] - width, cells.shape[dim], axis=dim)
        cells = jnp.concatenate(
            [
                lax.ppermute(tail, axis, [(i, (i + 1) % count) for i in range(ends)]),
                cells,
                lax.ppermute(head, axis, [((i + 1) % count, i) for i in range(ends)]),
            ],
            axis=dim,
        )
    return cells


def limited_slope(left_step, right_step):
    return (
        0.5
        * (jnp.sign(left_step) + jnp.sign(right_step))
        * jnp.minimum(jnp.abs(left_step), jnp.abs(right_step))
    )


def plm_divergence(values, speed, along_axis, extent):

    def take_range(source, offset_at, length):
        return lax.slice_in_dim(source, offset_at, offset_at + length, axis=along_axis)

    left_step = take_range(values, 1, extent + 2) - take_range(values, 0, extent + 2)
    right_step = take_range(values, 2, extent + 2) - take_range(values, 1, extent + 2)
    slopes = limited_slope(left_step, right_step)
    centre = take_range(values, 1, extent + 2)
    left_value = take_range(centre, 0, extent + 1) + 0.5 * take_range(slopes, 0, extent + 1)
    right_value = take_range(centre, 1, extent + 1) - 0.5 * take_range(slopes, 1, extent + 1)
    face_speed = 0.5 * (take_range(speed, 1, extent + 1) + take_range(speed, 2, extent + 1))
    face_flux = face_speed * 0.5 * (left_value + right_value) - 0.5 * (
        jnp.abs(face_speed) + sound_speed
    ) * (right_value - left_value)
    return take_range(face_flux, 1, extent) - take_range(face_flux, 0, extent)


def sector_roll(ring, quotient, remainder):
    sectors, per_member, rows, sector = ring.shape

    def kernel(quotient_ref, remainder_ref, ring_ref, out_ref):
        for i in range(per_member):
            whole = quotient_ref[i]
            part = remainder_ref[i]

            tile = 128
            tiles = sector // tile
            offset = part // tile
            within = part % tile
            lane = lax.broadcasted_iota(jnp.int32, (rows, tile), 1)

            def body(s, carry):
                current = ring_ref[(s - whole + sectors) % sectors, i]
                preceding = ring_ref[(s - whole - 1 + 2 * sectors) % sectors, i]
                window = [preceding[:, t * tile : (t + 1) * tile] for t in range(tiles)] + [
                    current[:, t * tile : (t + 1) * tile] for t in range(tiles)
                ]

                def pick(index):
                    chosen = window[index]
                    for back in range(1, tiles):
                        if index - back >= 0:
                            chosen = jnp.where(offset == back, window[index - back], chosen)
                    return chosen

                pieces = []
                for t in range(tiles):
                    upper = pltpu.roll(pick(tiles + t), within, 1)
                    lower = pltpu.roll(pick(tiles + t - 1), within, 1)
                    pieces.append(jnp.where(lane >= within, upper, lower))
                out_ref[s, i] = jnp.concatenate(pieces, axis=-1)
                return carry

            lax.fori_loop(0, sectors, body, 0)

    return pl.pallas_call(
        kernel,
        out_shape=jax.ShapeDtypeStruct(ring.shape, ring.dtype),
        in_specs=[
            pl.BlockSpec(memory_space=pltpu.SMEM),
            pl.BlockSpec(memory_space=pltpu.SMEM),
            pl.BlockSpec(memory_space=pltpu.VMEM),
        ],
        out_specs=pl.BlockSpec(memory_space=pltpu.VMEM),
    )(quotient, remainder, ring)


def minmod(a, b):
    return jnp.maximum(jnp.minimum(a, b), 0.0) + jnp.minimum(jnp.maximum(a, b), 0.0)

def face_divergence(v_m2, v_m1, v0, v_p1, v_p2, s_m1, s0, s_p1):
    slope_m1 = minmod(v_m1 - v_m2, v0 - v_m1)
    slope_0 = minmod(v0 - v_m1, v_p1 - v0)
    slope_p1 = minmod(v_p1 - v0, v_p2 - v_p1)
    def flux(left, right, w):
        return w * 0.5 * (left + right) - 0.5 * (jnp.abs(w) + 1.0) * (right - left)
    upper = flux(v0 + 0.5 * slope_0, v_p1 - 0.5 * slope_p1, 0.5 * (s0 + s_p1))
    lower = flux(v_m1 + 0.5 * slope_m1, v0 - 0.5 * slope_0, 0.5 * (s_m1 + s0))
    return upper - lower

def transport(dragged, speeds, radial_low, radial_high, ring_low, ring_high, rate_r, rate_a):
    fields, radii, layers, cells = dragged.shape

    def kernel(d_ref, s_ref, rl_ref, rh_ref, al_ref, ah_ref, out_ref):
        lane = lax.broadcasted_iota(jnp.int32, (layers, cells), 1)

        def edge_of(ref, f, component, *index):
            if f < fields:
                return ref[(f,) + index]
            density = ref[(0,) + index]
            safe = jnp.where(density == 0, 1.0, density)
            return jnp.where(density == 0, 0.0, ref[(component,) + index] / safe)

        def radial_at(f, r, offset):
            k = r + offset
            inner = d_ref[f, jnp.clip(k, 0, radii - 1)] if f < fields else s_ref[0, jnp.clip(k, 0, radii - 1)]
            low = edge_of(rl_ref, f, 1, jnp.clip(k + 2, 0, 1))
            high = edge_of(rh_ref, f, 1, jnp.clip(k - radii, 0, 1))
            return jnp.where(k < 0, low, jnp.where(k >= radii, high, inner))

        def ring_at(centre, f, r, offset):
            if offset < 0:
                moved = pltpu.roll(centre, -offset, 1)
                for j in range(-offset):
                    edge = edge_of(al_ref, f, 2, r, slice(None), slice(2 + offset + j, 3 + offset + j))
                    moved = jnp.where(lane == j, edge, moved)
            else:
                moved = pltpu.roll(centre, cells - offset, 1)
                for j in range(offset):
                    edge = edge_of(ah_ref, f, 2, r, slice(None), slice(j, j + 1))
                    moved = jnp.where(lane == cells - offset + j, edge, moved)
            return moved

        def body(r, carry):
            sr = s_ref[0, r]
            sa = s_ref[1, r]
            sr_m1 = radial_at(fields, r, -1)
            sr_p1 = radial_at(fields, r, 1)
            sa_m1 = ring_at(sa, fields + 1, r, -1)
            sa_p1 = ring_at(sa, fields + 1, r, 1)
            for f in range(fields):
                v0 = d_ref[f, r]
                radial = face_divergence(
                    radial_at(f, r, -2), radial_at(f, r, -1), v0, radial_at(f, r, 1), radial_at(f, r, 2),
                    sr_m1, sr, sr_p1,
                )
                azimuthal = face_divergence(
                    ring_at(v0, f, r, -2), ring_at(v0, f, r, -1), v0, ring_at(v0, f, r, 1), ring_at(v0, f, r, 2),
                    sa_m1, sa, sa_p1,
                )
                out_ref[f, r] = v0 - rate_r * radial - rate_a * azimuthal
            return carry

        lax.fori_loop(0, radii, body, 0)

    vmem = pl.BlockSpec(memory_space=pltpu.VMEM)
    return pl.pallas_call(
        kernel,
        out_shape=jax.ShapeDtypeStruct(dragged.shape, dragged.dtype),
        in_specs=[vmem] * 6,
        out_specs=vmem,
    )(dragged, speeds, radial_low, radial_high, ring_low, ring_high)


def local(
    gas_fields,
    orbit_shift,
    particle_velocity,
    particle_mass,
    particle_stop,
    particle_cell,
    particle_dest,
):
    field_count, radius_count, layers, sector = gas_fields.shape
    sectors = lax.axis_size("sec")
    per_member = radius_count // sectors
    member = lax.axis_index("sec")
    by_radius = gas_fields.transpose(1, 0, 2, 3)
    ring = lax.all_to_all(by_radius, "sec", split_axis=0, concat_axis=0, tiled=True)
    ring = ring.reshape(sectors, per_member, field_count * layers, sector)
    own_shift = lax.dynamic_slice_in_dim(orbit_shift, member * per_member, per_member)
    rolled = sector_roll(ring, own_shift // sector, own_shift % sector)
    rolled = rolled.reshape(sectors * per_member, field_count, layers, sector)
    shifted = lax.all_to_all(rolled, "sec", split_axis=0, concat_axis=0, tiled=True)
    shifted = shifted.transpose(1, 0, 2, 3)
    per_device = particle_dest.shape[0]
    devices = lax.axis_size(("rad", "sec"))
    capacity = 2 * per_device // devices
    target = particle_dest[:, 0]
    hits = target[:, None] == jnp.arange(devices, dtype=jnp.int32)[None, :]
    block_rows = min(128, per_device)
    block_count = per_device // block_rows
    hit_blocks = hits.astype(jnp.bfloat16).reshape(block_count, block_rows, devices)
    row_index = jnp.arange(block_rows, dtype=jnp.int32)
    within = (row_index[:, None] >= row_index[None, :]).astype(jnp.bfloat16)
    block_index = jnp.arange(block_count, dtype=jnp.int32)
    before = (block_index[:, None] > block_index[None, :]).astype(jnp.bfloat16)
    block_totals = jnp.sum(hit_blocks, axis=1, dtype=jnp.float32).astype(jnp.bfloat16)
    running = jnp.einsum(
        "ij,bjd->bid", within, hit_blocks, preferred_element_type=jnp.float32
    ) + jnp.dot(before, block_totals, preferred_element_type=jnp.float32)[:, None, :]
    running = running.reshape(per_device, devices)
    slot = jnp.sum(jnp.where(hits, running, 0.0), axis=1).astype(jnp.int32) - 1
    records = jnp.concatenate(
        [
            particle_velocity,
            particle_mass[None],
            particle_stop[None],
            particle_cell[None].astype(jnp.float32),
        ],
        axis=0,
    )
    slot_hot = slot[:, None] == jnp.arange(capacity, dtype=jnp.int32)[None, :]
    spread_records = jnp.where(slot_hot[:, None, :], records.T[:, :, None], 0.0).reshape(
        per_device, 6 * capacity
    )
    outbox = jnp.dot(
        hits.astype(jnp.float32).T, spread_records, precision=exact, preferred_element_type=jnp.float32
    ).reshape(devices, 6, capacity)
    outbox, _ = lax.optimization_barrier((outbox, ring))
    inbox = lax.all_to_all(outbox, ("rad", "sec"), split_axis=0, concat_axis=0, tiled=True)
    received = inbox.transpose(1, 0, 2).reshape(6, devices * capacity)
    row_count = radius_count * layers
    velocity_rows = (
        (shifted[1:4] / shifted[0:1])
        .reshape(3, row_count, sector)
        .transpose(1, 0, 2)
        .reshape(row_count, 3 * sector)
    )
    cells = received[5].astype(jnp.int32)
    row_hot = (
        (cells // sector)[:, None] == jnp.arange(row_count, dtype=jnp.int32)[None, :]
    ).astype(jnp.float32)
    azimuth_hot = (
        (cells % sector)[:, None] == jnp.arange(sector, dtype=jnp.int32)[None, :]
    ).astype(jnp.float32)
    picked = jnp.dot(
        row_hot, velocity_rows, precision=lax.Precision.HIGH, preferred_element_type=jnp.float32
    ).reshape(-1, 3, sector)
    local_speed = jnp.sum(picked * azimuth_hot[:, None, :], axis=2).T
    velocity_in = received[0:3]
    fraction = received[4] / (1.0 + received[4])
    change = (velocity_in - local_speed) * fraction[None]
    arrived_velocity = velocity_in - change
    impulse = received[3][None] * change
    spread = (impulse.T[:, :, None] * azimuth_hot[:, None, :]).reshape(-1, 3 * sector)
    deposit_rows = jnp.dot(row_hot.T, spread, precision=lax.Precision.HIGH, preferred_element_type=jnp.float32)
    momentum_added = (
        deposit_rows.reshape(row_count, 3, sector)
        .transpose(1, 0, 2)
        .reshape(3, radius_count, layers, sector)
    )
    dragged = jnp.concatenate([shifted[0:1], shifted[1:4] + momentum_added, shifted[4:5]], axis=0)
    radial_speed = dragged[1] / dragged[0]
    azimuthal_speed = dragged[2] / dragged[0]
    speeds = jnp.stack([radial_speed, azimuthal_speed], axis=0)
    rads = lax.axis_size("rad")
    radial_low = lax.ppermute(
        dragged[:, -2:],
        "rad",
        [(i, i + 1) for i in range(rads - 1)],
    )
    radial_high = lax.ppermute(
        dragged[:, :2],
        "rad",
        [(i + 1, i) for i in range(rads - 1)],
    )
    ring_low = lax.ppermute(
        dragged[..., -2:],
        "sec",
        [(i, (i + 1) % sectors) for i in range(sectors)],
    )
    ring_high = lax.ppermute(
        dragged[..., :2],
        "sec",
        [((i + 1) % sectors, i) for i in range(sectors)],
    )
    gas_next = transport(
        dragged, speeds, radial_low, radial_high, ring_low, ring_high, radial_rate, azimuth_rate
    )
    return (gas_next, arrived_velocity)


def solution(mesh):
    placed = (
        P(None, "rad", None, "sec"),
        P("rad"),
        P(None, ("rad", "sec")),
        P(("rad", "sec")),
        P(("rad", "sec")),
        P(("rad", "sec")),
        P(("rad", "sec"), None),
    )
    return jax.shard_map(
        local,
        mesh=mesh,
        in_specs=placed,
        out_specs=(P(None, "rad", None, "sec"), P(None, ("rad", "sec"))),
        check_vma=False,
    )
```

```python
import jax
import jax.numpy as jnp
from jax import lax
from jax.sharding import PartitionSpec as P
from jax.experimental import pallas as pl
from jax.experimental.pallas import tpu as pltpu

sound_speed = 1.0
radial_rate = 0.2
azimuth_rate = 0.2
exact = lax.Precision.HIGHEST


def passed_along(block, axis, distance):
    devices = range(lax.axis_size(axis))
    route = [((i - distance) % len(devices), i) for i in devices]
    return lax.ppermute(block, axis, route)


def with_halo(cells, sides, width, closed):
    for axis, dim in sides:
        count = lax.axis_size(axis)
        ends = count if closed else count - 1
        head = lax.slice_in_dim(cells, 0, width, axis=dim)
        tail = lax.slice_in_dim(cells, cells.shape[dim] - width, cells.shape[dim], axis=dim)
        cells = jnp.concatenate(
            [
                lax.ppermute(tail, axis, [(i, (i + 1) % count) for i in range(ends)]),
                cells,
                lax.ppermute(head, axis, [((i + 1) % count, i) for i in range(ends)]),
            ],
            axis=dim,
        )
    return cells


def limited_slope(left_step, right_step):
    return (
        0.5
        * (jnp.sign(left_step) + jnp.sign(right_step))
        * jnp.minimum(jnp.abs(left_step), jnp.abs(right_step))
    )


def plm_divergence(values, speed, along_axis, extent):

    def take_range(source, offset_at, length):
        return lax.slice_in_dim(source, offset_at, offset_at + length, axis=along_axis)

    left_step = take_range(values, 1, extent + 2) - take_range(values, 0, extent + 2)
    right_step = take_range(values, 2, extent + 2) - take_range(values, 1, extent + 2)
    slopes = limited_slope(left_step, right_step)
    centre = take_range(values, 1, extent + 2)
    left_value = take_range(centre, 0, extent + 1) + 0.5 * take_range(slopes, 0, extent + 1)
    right_value = take_range(centre, 1, extent + 1) - 0.5 * take_range(slopes, 1, extent + 1)
    face_speed = 0.5 * (take_range(speed, 1, extent + 1) + take_range(speed, 2, extent + 1))
    face_flux = face_speed * 0.5 * (left_value + right_value) - 0.5 * (
        jnp.abs(face_speed) + sound_speed
    ) * (right_value - left_value)
    return take_range(face_flux, 1, extent) - take_range(face_flux, 0, extent)


def sector_roll(ring, quotient, remainder):
    sectors, per_member, rows, sector = ring.shape

    def kernel(quotient_ref, remainder_ref, ring_ref, out_ref):
        for i in range(per_member):
            whole = quotient_ref[i]
            part = remainder_ref[i]

            tile = 128
            tiles = sector // tile
            offset = part // tile
            within = part % tile
            lane = lax.broadcasted_iota(jnp.int32, (rows, tile), 1)

            def body(s, carry):
                current = ring_ref[(s - whole + sectors) % sectors, i]
                preceding = ring_ref[(s - whole - 1 + 2 * sectors) % sectors, i]
                window = [preceding[:, t * tile : (t + 1) * tile] for t in range(tiles)] + [
                    current[:, t * tile : (t + 1) * tile] for t in range(tiles)
                ]

                def pick(index):
                    chosen = window[index]
                    for back in range(1, tiles):
                        if index - back >= 0:
                            chosen = jnp.where(offset == back, window[index - back], chosen)
                    return chosen

                pieces = []
                for t in range(tiles):
                    upper = pltpu.roll(pick(tiles + t), within, 1)
                    lower = pltpu.roll(pick(tiles + t - 1), within, 1)
                    pieces.append(jnp.where(lane >= within, upper, lower))
                out_ref[s, i] = jnp.concatenate(pieces, axis=-1)
                return carry

            lax.fori_loop(0, sectors, body, 0)

    return pl.pallas_call(
        kernel,
        out_shape=jax.ShapeDtypeStruct(ring.shape, ring.dtype),
        in_specs=[
            pl.BlockSpec(memory_space=pltpu.SMEM),
            pl.BlockSpec(memory_space=pltpu.SMEM),
            pl.BlockSpec(memory_space=pltpu.VMEM),
        ],
        out_specs=pl.BlockSpec(memory_space=pltpu.VMEM),
    )(quotient, remainder, ring)


def minmod(a, b):
    return jnp.maximum(jnp.minimum(a, b), 0.0) + jnp.minimum(jnp.maximum(a, b), 0.0)

def face_divergence(v_m2, v_m1, v0, v_p1, v_p2, s_m1, s0, s_p1):
    slope_m1 = minmod(v_m1 - v_m2, v0 - v_m1)
    slope_0 = minmod(v0 - v_m1, v_p1 - v0)
    slope_p1 = minmod(v_p1 - v0, v_p2 - v_p1)
    def flux(left, right, w):
        return w * 0.5 * (left + right) - 0.5 * (jnp.abs(w) + 1.0) * (right - left)
    upper = flux(v0 + 0.5 * slope_0, v_p1 - 0.5 * slope_p1, 0.5 * (s0 + s_p1))
    lower = flux(v_m1 + 0.5 * slope_m1, v0 - 0.5 * slope_0, 0.5 * (s_m1 + s0))
    return upper - lower

def transport(dragged, radial_low, radial_high, ring_low, ring_high, rate_r, rate_a):
    fields, radii, layers, cells = dragged.shape

    def kernel(d_ref, rl_ref, rh_ref, al_ref, ah_ref, out_ref):
        lane = lax.broadcasted_iota(jnp.int32, (layers, cells), 1)

        def edge_of(ref, f, component, *index):
            if f < fields:
                return ref[(f,) + index]
            density = ref[(0,) + index]
            safe = jnp.where(density == 0, 1.0, density)
            return jnp.where(density == 0, 0.0, ref[(component,) + index] / safe)

        def radial_at(f, r, offset):
            k = r + offset
            inner = d_ref[f, jnp.clip(k, 0, radii - 1)] if f < fields else d_ref[1, jnp.clip(k, 0, radii - 1)] / d_ref[0, jnp.clip(k, 0, radii - 1)]
            low = edge_of(rl_ref, f, 1, jnp.clip(k + 2, 0, 1))
            high = edge_of(rh_ref, f, 1, jnp.clip(k - radii, 0, 1))
            return jnp.where(k < 0, low, jnp.where(k >= radii, high, inner))

        def ring_at(centre, f, r, offset):
            if offset < 0:
                moved = pltpu.roll(centre, -offset, 1)
                for j in range(-offset):
                    edge = edge_of(al_ref, f, 2, r, slice(None), slice(2 + offset + j, 3 + offset + j))
                    moved = jnp.where(lane == j, edge, moved)
            else:
                moved = pltpu.roll(centre, cells - offset, 1)
                for j in range(offset):
                    edge = edge_of(ah_ref, f, 2, r, slice(None), slice(j, j + 1))
                    moved = jnp.where(lane == cells - offset + j, edge, moved)
            return moved

        def body(r, carry):
            sr = d_ref[1, r] / d_ref[0, r]
            sa = d_ref[2, r] / d_ref[0, r]
            sr_m1 = radial_at(fields, r, -1)
            sr_p1 = radial_at(fields, r, 1)
            sa_m1 = ring_at(sa, fields + 1, r, -1)
            sa_p1 = ring_at(sa, fields + 1, r, 1)
            for f in range(fields):
                v0 = d_ref[f, r]
                radial = face_divergence(
                    radial_at(f, r, -2), radial_at(f, r, -1), v0, radial_at(f, r, 1), radial_at(f, r, 2),
                    sr_m1, sr, sr_p1,
                )
                azimuthal = face_divergence(
                    ring_at(v0, f, r, -2), ring_at(v0, f, r, -1), v0, ring_at(v0, f, r, 1), ring_at(v0, f, r, 2),
                    sa_m1, sa, sa_p1,
                )
                out_ref[f, r] = v0 - rate_r * radial - rate_a * azimuthal
            return carry

        lax.fori_loop(0, radii, body, 0)

    vmem = pl.BlockSpec(memory_space=pltpu.VMEM)
    return pl.pallas_call(
        kernel,
        out_shape=jax.ShapeDtypeStruct(dragged.shape, dragged.dtype),
        in_specs=[vmem] * 5,
        out_specs=vmem,
    )(dragged, radial_low, radial_high, ring_low, ring_high)


def local(
    gas_fields,
    orbit_shift,
    particle_velocity,
    particle_mass,
    particle_stop,
    particle_cell,
    particle_dest,
):
    field_count, radius_count, layers, sector = gas_fields.shape
    sectors = lax.axis_size("sec")
    per_member = radius_count // sectors
    member = lax.axis_index("sec")
    by_radius = gas_fields.transpose(1, 0, 2, 3)
    ring = lax.all_to_all(by_radius, "sec", split_axis=0, concat_axis=0, tiled=True)
    ring = ring.reshape(sectors, per_member, field_count * layers, sector)
    own_shift = lax.dynamic_slice_in_dim(orbit_shift, member * per_member, per_member)
    rolled = sector_roll(ring, own_shift // sector, own_shift % sector)
    rolled = rolled.reshape(sectors * per_member, field_count, layers, sector)
    shifted = lax.all_to_all(rolled, "sec", split_axis=0, concat_axis=0, tiled=True)
    shifted = shifted.transpose(1, 0, 2, 3)
    per_device = particle_dest.shape[0]
    devices = lax.axis_size(("rad", "sec"))
    capacity = 2 * per_device // devices
    target = particle_dest[:, 0]
    hits = target[:, None] == jnp.arange(devices, dtype=jnp.int32)[None, :]
    block_rows = min(128, per_device)
    block_count = per_device // block_rows
    hit_blocks = hits.astype(jnp.bfloat16).reshape(block_count, block_rows, devices)
    row_index = jnp.arange(block_rows, dtype=jnp.int32)
    within = (row_index[:, None] >= row_index[None, :]).astype(jnp.bfloat16)
    block_index = jnp.arange(block_count, dtype=jnp.int32)
    before = (block_index[:, None] > block_index[None, :]).astype(jnp.bfloat16)
    block_totals = jnp.sum(hit_blocks, axis=1, dtype=jnp.float32).astype(jnp.bfloat16)
    running = jnp.einsum(
        "ij,bjd->bid", within, hit_blocks, preferred_element_type=jnp.float32
    ) + jnp.dot(before, block_totals, preferred_element_type=jnp.float32)[:, None, :]
    running = running.reshape(per_device, devices)
    slot = jnp.sum(jnp.where(hits, running, 0.0), axis=1).astype(jnp.int32) - 1
    records = jnp.concatenate(
        [
            particle_velocity,
            particle_mass[None],
            particle_stop[None],
            particle_cell[None].astype(jnp.float32),
        ],
        axis=0,
    )
    slot_hot = slot[:, None] == jnp.arange(capacity, dtype=jnp.int32)[None, :]
    spread_records = jnp.where(slot_hot[:, None, :], records.T[:, :, None], 0.0).reshape(
        per_device, 6 * capacity
    )
    outbox = jnp.dot(
        hits.astype(jnp.float32).T, spread_records, precision=exact, preferred_element_type=jnp.float32
    ).reshape(devices, 6, capacity)
    outbox, _ = lax.optimization_barrier((outbox, ring))
    inbox = lax.all_to_all(outbox, ("rad", "sec"), split_axis=0, concat_axis=0, tiled=True)
    received = inbox.transpose(1, 0, 2).reshape(6, devices * capacity)
    row_count = radius_count * layers
    velocity_rows = (
        (shifted[1:4] / shifted[0:1])
        .reshape(3, row_count, sector)
        .transpose(1, 0, 2)
        .reshape(row_count, 3 * sector)
    )
    cells = received[5].astype(jnp.int32)
    row_hot = (
        (cells // sector)[:, None] == jnp.arange(row_count, dtype=jnp.int32)[None, :]
    ).astype(jnp.float32)
    azimuth_hot = (
        (cells % sector)[:, None] == jnp.arange(sector, dtype=jnp.int32)[None, :]
    ).astype(jnp.float32)
    picked = jnp.dot(
        row_hot, velocity_rows, precision=lax.Precision.HIGH, preferred_element_type=jnp.float32
    ).reshape(-1, 3, sector)
    local_speed = jnp.sum(picked * azimuth_hot[:, None, :], axis=2).T
    velocity_in = received[0:3]
    fraction = received[4] / (1.0 + received[4])
    change = (velocity_in - local_speed) * fraction[None]
    arrived_velocity = velocity_in - change
    impulse = received[3][None] * change
    spread = (impulse.T[:, :, None] * azimuth_hot[:, None, :]).reshape(-1, 3 * sector)
    deposit_rows = jnp.dot(row_hot.T, spread, precision=lax.Precision.HIGH, preferred_element_type=jnp.float32)
    momentum_added = (
        deposit_rows.reshape(row_count, 3, sector)
        .transpose(1, 0, 2)
        .reshape(3, radius_count, layers, sector)
    )
    dragged = jnp.concatenate([shifted[0:1], shifted[1:4] + momentum_added, shifted[4:5]], axis=0)
    rads = lax.axis_size("rad")
    radial_low = lax.ppermute(
        dragged[:, -2:],
        "rad",
        [(i, i + 1) for i in range(rads - 1)],
    )
    radial_high = lax.ppermute(
        dragged[:, :2],
        "rad",
        [(i + 1, i) for i in range(rads - 1)],
    )
    ring_low = lax.ppermute(
        dragged[..., -2:],
        "sec",
        [(i, (i + 1) % sectors) for i in range(sectors)],
    )
    ring_high = lax.ppermute(
        dragged[..., :2],
        "sec",
        [((i + 1) % sectors, i) for i in range(sectors)],
    )
    gas_next = transport(
        dragged, radial_low, radial_high, ring_low, ring_high, radial_rate, azimuth_rate
    )
    return (gas_next, arrived_velocity)


def solution(mesh):
    placed = (
        P(None, "rad", None, "sec"),
        P("rad"),
        P(None, ("rad", "sec")),
        P(("rad", "sec")),
        P(("rad", "sec")),
        P(("rad", "sec")),
        P(("rad", "sec"), None),
    )
    return jax.shard_map(
        local,
        mesh=mesh,
        in_specs=placed,
        out_specs=(P(None, "rad", None, "sec"), P(None, ("rad", "sec"))),
        check_vma=False,
    )
```
